256 devices in a mesh: dp: 2 (over y_hi), retr: 16 (over x, y_lo, core), tensor: 8 (over z).
Axes of the slice: x: 4, y: 4 (y_hi: 2, y_lo: 2; y = y_hi * 2 + y_lo), z: 8, core: 2. Of those that a mesh axis runs over, the one named last changes fastest.
Arguments:
- hidden_in: bfloat16 [16384, 4096], P(('dp', 'retr'), 'tensor'), may hold values from -12 to 12
- norm_gain: float32 [4096], replicated, may hold values from 0.1 to 1.9
- nbr_table: int32 [256, 2], P(('dp', 'retr')), may hold values from 0 to 63, as said below
- encodings: bfloat16 [64, 128, 1024], P('retr'), may hold values from -21 to 21
- enc_mask: int32 [64, 4], P('retr'), may hold values from 0 to 1, as said below
- w_query: bfloat16 [4096, 4096], P(None, 'tensor'), may hold values from -0.02703125 to 0.02703125
- w_key: bfloat16 [1024, 4096], P(None, 'tensor'), may hold values from -0.1021875 to 0.1021875
- w_value: bfloat16 [1024, 4096], P(None, 'tensor'), may hold values from -0.1875 to 0.1875
- w_out: bfloat16 [4096, 4096], P('tensor'), may hold values from -0.125 to 0.125
Outputs:
- mixed: bfloat16 [16384, 4096], P(('dp', 'retr'), 'tensor')
The draws below stay inside these ranges and needn't reach their ends.
Inputs may be any that keep to these rules, and one draw needn't show every extreme that they name: `nbr_table`: each aligned block of 8 table rows (the rows of one device) holds 16 distinct ids; at most 2 of them share the value id // 4, and in every block some value of id // 4 has exactly 2. `enc_mask`: in each row the ones come first; the first entry is 1.
All inputs are finite; a program needn't handle non-finite values.
Results may differ from the reference program's by a relative error of at most 0.012.
The reference program's roundings to bfloat16 on the way (of `normed`, `queries`, `probs` and `attended`) count: a program that leaves them out, or rounds other values in their place, can miss the bound.
Values may be sent and summed in bfloat16 or wider, within the bound.
No kernel may reach another device: no remote copies, remote signals or barrier semaphores. Data moves between devices by JAX's collectives and lax.ppermute only.
A program may use at most 128 MiB of HBM per device.

```python
import math
import jax
import jax.numpy as jnp
from jax import lax

D = 4096
H = 32
HD = 128
E = 1024
SEG = 64
NBRS = 2
NBR_LEN = 128
BLOCK = 32
TOK_DEV = 512
NB_DEV = 4
TOKENS = 16384
SEGMENTS = 256
NB = 64
NBLK = 4
NEED = 16
CAP = 2
N_RETR = 16


def query_columns(key):
    return jax.random.uniform(jax.random.fold_in(key, 101), (E, H * HD), jnp.float32, -1.73, 1.73)


def draw_w_query(key, part):
    upper = query_columns(key)
    lower = jax.random.uniform(jax.random.fold_in(key, 102), (D - E, H * HD), jnp.float32, -1.73, 1.73)
    return (jnp.concatenate([upper, lower], axis=0) * D ** (-0.5)).astype(jnp.bfloat16)


def draw_w_key(key, part):
    own_part = jax.random.uniform(jax.random.fold_in(key, 103), (E, H * HD), jnp.float32, -1.73, 1.73)
    return (own_part * E ** (-0.5)).astype(jnp.bfloat16)


def draw_hidden_in(key, part):
    key_a, key_b = jax.random.split(key, 2)
    values = jnp.clip(jax.random.normal(key_a, (TOKENS, D), jnp.float32), -4.0, 4.0)
    row_scale = jnp.exp(jax.random.uniform(key_b, (TOKENS, 1), jnp.float32, jnp.log(0.3), jnp.log(3.0)))
    return (values * row_scale).astype(jnp.bfloat16)


def draw_encodings(key, part):
    key_a = jax.random.fold_in(key, 0)
    values = jnp.clip(jax.random.normal(key_a, (NB, NBR_LEN, E), jnp.float32), -4.0, 4.0)
    return values.astype(jnp.bfloat16)


def draw_enc_mask(key, part):
    counts_live = jax.random.randint(key, (NB, 1), 1, NBLK + 1)
    return (jnp.arange(NBLK, dtype=jnp.int32)[None, :] < counts_live).astype(jnp.int32)


def draw_nbr_table(key, part):
    slots_all = N_RETR * CAP

    def one_device(device_key):
        key_a, key_b, key_c, key_d = jax.random.split(device_key, 4)
        full_owner = jax.random.randint(key_a, (), 0, N_RETR)
        slot_ids = jnp.arange(slots_all, dtype=jnp.int32)
        owner_of = slot_ids // CAP
        copy_of = slot_ids % CAP
        ranking = jax.random.permutation(key_b, slots_all).astype(jnp.int32)
        priority = jnp.where(owner_of == full_owner, ranking - slots_all, ranking)
        picked = jnp.argsort(priority, stable=True)[:NEED]
        offset_of = jax.random.randint(key_c, (N_RETR,), 0, NB_DEV)
        chosen_owner = owner_of[picked]
        local_slot = (offset_of[chosen_owner] + copy_of[picked]) % NB_DEV
        entry_ids = chosen_owner * NB_DEV + local_slot
        mixing = jax.random.permutation(key_d, NEED)
        return entry_ids[mixing].astype(jnp.int32)
    device_keys = jax.random.split(key, TOKENS // TOK_DEV)
    return jax.vmap(one_device)(device_keys).reshape(SEGMENTS, NBRS)


def with_spikes(values, own_key, source, target, shards_of, factor):
    def block_of(position):
        return (jnp.arange(values.shape[position]) // (values.shape[position] // shards_of)).reshape((-1,) + (1,) * (values.ndim - 1 - position))

    one_side = jax.random.permutation(own_key, shards_of)[block_of(target)]
    second = (block_of(target) + shards_of // 2) % shards_of
    return jnp.where((block_of(source) == one_side) | (block_of(source) == second), factor * values, values)


def level_of(own_key, shape, cuts, least, largest):
    def one(axis_at, parts):
        steps = jax.random.uniform(jax.random.fold_in(jax.random.fold_in(own_key, 6), axis_at), (parts,), jnp.float32, least / len(cuts), largest / len(cuts))
        return jnp.repeat(jnp.exp(steps), shape[axis_at] // parts).reshape((-1,) + (1,) * (len(shape) - axis_at - 1))

    level = one(*cuts[0])
    for cut in cuts[1:]:
        level = level * one(*cut)
    return level


def normal_values(key, dims, scale, reach, shards=(), kind=jnp.bfloat16):
    values = jax.random.normal(key, dims, jnp.float32) * scale
    if len(shards) > 0:
        values = level_of(key, dims, shards, -0.22, 0.18) * values
    return jnp.clip(values, min=-reach, max=reach).astype(kind)


def bell_draw_with(rng, shape, scale, bound, shards, heavy, held_as=jnp.bfloat16):
    entries = scale * jax.random.normal(rng, shape, jnp.float32)
    if shards:
        entries = entries * level_of(rng, shape, shards, -0.22, 0.18)
    return jnp.clip(with_spikes(entries, jax.random.fold_in(rng, 3), *heavy), -bound, bound).astype(held_as)


def setup_inputs(seed: int = 0) -> dict:
    arg_keys = jax.random.split(jax.random.key(seed), 10)
    hidden_in = draw_hidden_in(jax.random.fold_in(arg_keys[9], 71), 0)
    norm_gain = jnp.clip(1.0 + 0.18 * jax.random.normal(arg_keys[1], (D,), jnp.float32), 0.1, 1.9)
    nbr_table = draw_nbr_table(jax.random.fold_in(arg_keys[9], 71), 0)
    encodings = draw_encodings(jax.random.fold_in(arg_keys[9], 71), 0)
    enc_mask = draw_enc_mask(jax.random.fold_in(arg_keys[9], 71), 0)
    w_query = draw_w_query(jax.random.fold_in(arg_keys[9], 71), 0)
    w_key = draw_w_key(jax.random.fold_in(arg_keys[9], 71), 0)
    w_value = normal_values(arg_keys[7], (E, H * HD), E ** -0.5, 0.1875, ((1, 8),))
    w_out = bell_draw_with(arg_keys[8], (H * HD, D), (H * HD) ** -0.5, 0.125, ((0, 8),), (0, 1, 8, 2.0))
    return dict(hidden_in=hidden_in, norm_gain=norm_gain, nbr_table=nbr_table, encodings=encodings, enc_mask=enc_mask, w_query=w_query, w_key=w_key, w_value=w_value, w_out=w_out)


def reference(hidden_in, norm_gain, nbr_table, encodings, enc_mask, w_query, w_key, w_value, w_out):
    widened = hidden_in.astype(jnp.float32)
    mean_sq = lax.optimization_barrier(jnp.mean(widened * widened, axis=-1, keepdims=True))
    normed = (widened * lax.rsqrt(mean_sq + 1e-05) * norm_gain).astype(jnp.bfloat16)
    queries = jnp.dot(normed, w_query, preferred_element_type=jnp.float32).astype(jnp.bfloat16)
    flat_enc = encodings.reshape(NB * NBR_LEN, E)
    enc_keys = jnp.dot(flat_enc, w_key, preferred_element_type=jnp.float32).astype(jnp.bfloat16)
    enc_values = jnp.dot(flat_enc, w_value, preferred_element_type=jnp.float32).astype(jnp.bfloat16)
    enc_keys = enc_keys.reshape(NB, NBR_LEN, H, HD)
    enc_values = enc_values.reshape(NB, NBR_LEN, H, HD)
    token_live = jnp.repeat(enc_mask, BLOCK, axis=1)
    query_blocks = queries.reshape(SEGMENTS, SEG, H, HD)
    factor = 1.0 / math.sqrt(HD)

    def one_segment(inputs):
        query_rows, entry_ids = inputs
        key_rows = enc_keys[entry_ids].reshape(NBRS * NBR_LEN, H, HD).astype(jnp.float32)
        value_rows = enc_values[entry_ids].reshape(NBRS * NBR_LEN, H, HD).astype(jnp.float32)
        key_live = token_live[entry_ids].reshape(NBRS * NBR_LEN) > 0
        scores = jnp.einsum('qhd,khd->hqk', query_rows.astype(jnp.float32), key_rows) * factor
        scores = jnp.where(key_live[None, None, :], scores, -1e+30)
        row_max = lax.optimization_barrier(jnp.max(scores, axis=-1, keepdims=True))
        weights = jnp.exp(scores - row_max) * key_live[None, None, :].astype(jnp.float32)
        probs = (weights / lax.optimization_barrier(jnp.sum(weights, axis=-1, keepdims=True))).astype(jnp.bfloat16)
        attended = jnp.einsum('hqk,khd->qhd', probs.astype(jnp.float32), value_rows)
        return attended.astype(jnp.bfloat16).reshape(SEG, H * HD)
    attended = lax.map(one_segment, (query_blocks, nbr_table)).reshape(TOKENS, H * HD)
    projected = jnp.dot(attended, w_out, preferred_element_type=jnp.float32)
    return (widened + projected).astype(jnp.bfloat16)
```

```python
import math

import jax
import jax.numpy as jnp
from jax import lax
from jax.sharding import PartitionSpec as P

HD = 128
NBRS = 2
BLOCK = 32
CAP = 2


def attend_gathered(queries, key_value, selected_marks, segment_count, head_cols):
    tok_rows = queries.shape[0]
    head_count = head_cols // HD
    entry_keys = key_value.shape[0] // segment_count * key_value.shape[1]
    mask_cols = selected_marks.shape[1]
    key_block = key_value[:, :, :head_cols].reshape(segment_count, entry_keys, head_count, HD)
    value_block = key_value[:, :, head_cols:].reshape(segment_count, entry_keys, head_count, HD)
    key_live = (
        jnp.repeat(selected_marks.reshape(segment_count, NBRS * mask_cols), BLOCK, axis=1) > 0
    )
    query_block = queries.reshape(segment_count, tok_rows // segment_count, head_count, HD)
    factor = 1.0 / math.sqrt(HD)
    scores = (
        jnp.einsum("cqhd,ckhd->chqk", query_block, key_block, preferred_element_type=jnp.float32)
        * factor
    )
    key_open = key_live[:, None, None, :]
    scores = jnp.where(key_open, scores, -1e30)
    row_max = jnp.max(scores, axis=-1, keepdims=True)
    weights = jnp.exp(scores - row_max) * key_open.astype(jnp.float32)
    probabilities = (weights / jnp.sum(weights, axis=-1, keepdims=True)).astype(jnp.bfloat16)
    attended = jnp.einsum(
        "chqk,ckhd->cqhd", probabilities, value_block, preferred_element_type=jnp.float32
    )
    return attended.astype(jnp.bfloat16).reshape(tok_rows, head_cols)


def local(hidden_in, norm_gain, nbr_table, encodings, enc_mask, w_query, w_key, w_value, w_out):
    segment_count = nbr_table.shape[0]
    nb_dev, entry_len, enc_width = encodings.shape
    mask_cols = enc_mask.shape[1]
    head_cols = w_key.shape[1]
    wanted = nbr_table.reshape(-1)
    need_count = wanted.shape[0]

    info = jnp.concatenate([wanted, enc_mask.reshape(-1)])
    all_info = lax.all_gather(info, "retr", axis=0, tiled=False)
    retr_count = all_info.shape[0]
    all_wanted = all_info[:, :need_count]
    all_marks = all_info[:, need_count:].reshape(retr_count * nb_dev, mask_cols)

    gathered = lax.all_gather(hidden_in, "tensor", axis=1, tiled=True)

    w_both = jnp.concatenate([w_key, w_value], axis=1)
    own_kv = jnp.dot(
        encodings.reshape(nb_dev * entry_len, enc_width), w_both, preferred_element_type=jnp.float32
    ).astype(jnp.bfloat16).reshape(nb_dev, entry_len * 2 * head_cols)

    me = lax.axis_index("retr")
    mine = (all_wanted // nb_dev) == me
    rank = jnp.cumsum(mine.astype(jnp.int32), axis=1) - 1
    slot_ids = jnp.arange(CAP, dtype=jnp.int32)
    chosen = mine[:, None, :] & (rank[:, None, :] == slot_ids[None, :, None])
    local_idx = jnp.sum(jnp.where(chosen, all_wanted[:, None, :] % nb_dev, 0), axis=2)
    pick = (local_idx[:, :, None] == jnp.arange(nb_dev, dtype=jnp.int32)).astype(jnp.bfloat16)
    send = jnp.einsum(
        "qjn,nf->qjf", pick, own_kv, preferred_element_type=jnp.float32
    ).astype(jnp.bfloat16)
    recv = lax.all_to_all(send, "retr", 0, 0, tiled=True)

    owner = wanted // nb_dev
    same = owner[:, None] == owner[None, :]
    earlier = jnp.arange(need_count)[None, :] < jnp.arange(need_count)[:, None]
    my_rank = jnp.sum((same & earlier).astype(jnp.int32), axis=1)
    flat_idx = owner * CAP + my_rank
    key_value = jnp.take(recv.reshape(retr_count * CAP, -1), flat_idx, axis=0)
    key_value = key_value.reshape(need_count, entry_len, 2 * head_cols)
    picked_marks = jnp.take(all_marks, wanted, axis=0)

    widened = gathered.astype(jnp.float32)
    mean_sq = jnp.mean(widened * widened, axis=-1, keepdims=True)
    normed = (widened * lax.rsqrt(mean_sq + 1e-05) * norm_gain).astype(jnp.bfloat16)
    queries = jnp.dot(normed, w_query, preferred_element_type=jnp.float32).astype(jnp.bfloat16)

    attended = attend_gathered(queries, key_value, picked_marks, segment_count, head_cols)
    partial_value = jnp.dot(attended, w_out, preferred_element_type=jnp.float32)
    summed = lax.psum_scatter(
        partial_value.astype(jnp.bfloat16), "tensor", scatter_dimension=1, tiled=True
    )
    return (hidden_in.astype(jnp.float32) + summed.astype(jnp.float32)).astype(jnp.bfloat16)


def solution(mesh):
    in_specs = (
        P(("dp", "retr"), "tensor"),
        P(),
        P(("dp", "retr"), None),
        P("retr", None, None),
        P("retr", None),
        P(None, "tensor"),
        P(None, "tensor"),
        P(None, "tensor"),
        P("tensor", None),
    )
    out_specs = P(("dp", "retr"), "tensor")
    return jax.shard_map(local, mesh=mesh, in_specs=in_specs, out_specs=out_specs, check_vma=False)
```

```python
import math

import jax
import jax.numpy as jnp
from jax import lax
from jax.experimental import pallas as pl
from jax.experimental.pallas import tpu as pltpu
from jax.sharding import PartitionSpec as P

HD = 128
NBRS = 2
BLOCK = 32
CAP = 2


def attend_kernel(flat_ref, marks_ref, q_ref, kv0_ref, kv1_ref, o_ref):
    seg = pl.program_id(0)
    head_cols = q_ref.shape[1]
    entry_len = kv0_ref.shape[1]
    mask_cols = marks_ref.shape[0] // flat_ref.shape[0]
    factor = 1.0 / math.sqrt(HD)
    block_of = lax.broadcasted_iota(jnp.int32, (1, entry_len), 1) // BLOCK

    def live_of(entry):
        live = jnp.zeros((1, entry_len), jnp.float32)
        for b in range(mask_cols):
            mark = marks_ref[entry * mask_cols + b].astype(jnp.float32)
            live = jnp.where(block_of == b, mark, live)
        return live

    live0 = live_of(seg * NBRS)
    live1 = live_of(seg * NBRS + 1)
    open0 = live0 > 0
    open1 = live1 > 0
    nt = (((1,), (1,)), ((), ()))
    for h in range(head_cols // HD):
        cols = slice(h * HD, (h + 1) * HD)
        vcols = slice(head_cols + h * HD, head_cols + (h + 1) * HD)
        qh = q_ref[:, cols]
        s0 = lax.dot_general(qh, kv0_ref[0, :, cols], nt, preferred_element_type=jnp.float32) * factor
        s1 = lax.dot_general(qh, kv1_ref[0, :, cols], nt, preferred_element_type=jnp.float32) * factor
        s0 = jnp.where(open0, s0, -1e30)
        s1 = jnp.where(open1, s1, -1e30)
        row_max = jnp.maximum(jnp.max(s0, axis=-1, keepdims=True), jnp.max(s1, axis=-1, keepdims=True))
        w0 = jnp.exp(s0 - row_max) * live0
        w1 = jnp.exp(s1 - row_max) * live1
        total = jnp.sum(w0, axis=-1, keepdims=True) + jnp.sum(w1, axis=-1, keepdims=True)
        p0 = (w0 / total).astype(jnp.bfloat16)
        p1 = (w1 / total).astype(jnp.bfloat16)
        att = jnp.dot(p0, kv0_ref[0, :, vcols], preferred_element_type=jnp.float32)
        att = att + jnp.dot(p1, kv1_ref[0, :, vcols], preferred_element_type=jnp.float32)
        o_ref[:, cols] = att.astype(o_ref.dtype)


def attend(flat_idx, marks, queries, slots):
    tok_rows, head_cols = queries.shape
    segment_count = flat_idx.shape[0] // NBRS
    seg_rows = tok_rows // segment_count
    entry_len, kv_cols = slots.shape[1], slots.shape[2]
    grid_spec = pltpu.PrefetchScalarGridSpec(
        num_scalar_prefetch=2,
        grid=(segment_count,),
        in_specs=[
            pl.BlockSpec((seg_rows, head_cols), lambda s, f, m: (s, 0)),
            pl.BlockSpec((1, entry_len, kv_cols), lambda s, f, m: (f[s * NBRS], 0, 0)),
            pl.BlockSpec((1, entry_len, kv_cols), lambda s, f, m: (f[s * NBRS + 1], 0, 0)),
        ],
        out_specs=pl.BlockSpec((seg_rows, head_cols), lambda s, f, m: (s, 0)),
    )
    return pl.pallas_call(
        attend_kernel,
        out_shape=jax.ShapeDtypeStruct((tok_rows, head_cols), jnp.bfloat16),
        grid_spec=grid_spec,
    )(flat_idx, marks, queries, slots, slots)


def local(hidden_in, norm_gain, nbr_table, encodings, enc_mask, w_query, w_key, w_value, w_out):
    segment_count = nbr_table.shape[0]
    nb_dev, entry_len, enc_width = encodings.shape
    mask_cols = enc_mask.shape[1]
    head_cols = w_key.shape[1]
    wanted = nbr_table.reshape(-1)
    need_count = wanted.shape[0]

    info = jnp.concatenate([wanted, enc_mask.reshape(-1)]).astype(jnp.float32)
    all_info = lax.all_gather(info, "retr", axis=0, tiled=False).astype(jnp.int32)
    retr_count = all_info.shape[0]
    all_wanted = all_info[:, :need_count]
    all_marks = all_info[:, need_count:].reshape(retr_count * nb_dev, mask_cols)

    gathered = lax.all_gather(hidden_in, "tensor", axis=1, tiled=True)

    w_both = jnp.concatenate([w_key, w_value], axis=1)
    own_kv = jnp.dot(
        encodings.reshape(nb_dev * entry_len, enc_width), w_both, preferred_element_type=jnp.float32
    ).astype(jnp.bfloat16).reshape(nb_dev, entry_len, 2 * head_cols)

    me = lax.axis_index("retr")
    mine = (all_wanted // nb_dev) == me
    rank = jnp.cumsum(mine.astype(jnp.int32), axis=1) - 1
    slot_ids = jnp.arange(CAP, dtype=jnp.int32)
    chosen = mine[:, None, :] & (rank[:, None, :] == slot_ids[None, :, None])
    local_idx = jnp.sum(jnp.where(chosen, all_wanted[:, None, :] % nb_dev, 0), axis=2)
    send = jnp.take(own_kv, local_idx.reshape(-1), axis=0)
    send = send.reshape(retr_count, CAP * entry_len, 2 * head_cols)
    recv = lax.all_to_all(send, "retr", 0, 0, tiled=True)
    slots = recv.reshape(retr_count * CAP, entry_len, 2 * head_cols)

    owner = wanted // nb_dev
    same = owner[:, None] == owner[None, :]
    earlier = jnp.arange(need_count)[None, :] < jnp.arange(need_count)[:, None]
    my_rank = jnp.sum((same & earlier).astype(jnp.int32), axis=1)
    flat_idx = owner * CAP + my_rank
    picked_marks = jnp.take(all_marks, wanted, axis=0).reshape(-1)

    widened = gathered.astype(jnp.float32)
    mean_sq = jnp.mean(widened * widened, axis=-1, keepdims=True)
    normed = (widened * lax.rsqrt(mean_sq + 1e-05) * norm_gain).astype(jnp.bfloat16)
    queries = jnp.dot(normed, w_query, preferred_element_type=jnp.float32).astype(jnp.bfloat16)

    attended = attend(flat_idx, picked_marks, queries, slots)
    partial_value = jnp.dot(attended, w_out, preferred_element_type=jnp.float32)
    summed = lax.psum_scatter(
        partial_value.astype(jnp.bfloat16), "tensor", scatter_dimension=1, tiled=True
    )
    return (hidden_in.astype(jnp.float32) + summed.astype(jnp.float32)).astype(jnp.bfloat16)


def solution(mesh):
    in_specs = (
        P(("dp", "retr"), "tensor"),
        P(),
        P(("dp", "retr"), None),
        P("retr", None, None),
        P("retr", None),
        P(None, "tensor"),
        P(None, "tensor"),
        P(None, "tensor"),
        P("tensor", None),
    )
    out_specs = P(("dp", "retr"), "tensor")
    return jax.shard_map(local, mesh=mesh, in_specs=in_specs, out_specs=out_specs, check_vma=False)
```

```python
import functools
import math

import jax
import jax.numpy as jnp
from jax import lax
from jax.experimental import pallas as pl
from jax.experimental.pallas import tpu as pltpu
from jax.sharding import PartitionSpec as P

HD = 128
NBRS = 2
BLOCK = 32
CAP = 2


def attend_kernel(flat_ref, q_ref, kv0_ref, kv1_ref, o_ref, *, entry_len):
    head_cols = q_ref.shape[1]
    factor = 1.0 / math.sqrt(HD)
    live0 = kv0_ref[0, entry_len:entry_len + 1, :entry_len].astype(jnp.float32)
    live1 = kv1_ref[0, entry_len:entry_len + 1, :entry_len].astype(jnp.float32)
    open0 = live0 > 0
    open1 = live1 > 0
    nt = (((1,), (1,)), ((), ()))
    for h in range(head_cols // HD):
        cols = slice(h * HD, (h + 1) * HD)
        vcols = slice(head_cols + h * HD, head_cols + (h + 1) * HD)
        qh = q_ref[:, cols]
        s0 = lax.dot_general(qh, kv0_ref[0, :entry_len, cols], nt, preferred_element_type=jnp.float32) * factor
        s1 = lax.dot_general(qh, kv1_ref[0, :entry_len, cols], nt, preferred_element_type=jnp.float32) * factor
        s0 = jnp.where(open0, s0, -1e30)
        s1 = jnp.where(open1, s1, -1e30)
        row_max = jnp.maximum(jnp.max(s0, axis=-1, keepdims=True), jnp.max(s1, axis=-1, keepdims=True))
        w0 = jnp.exp(s0 - row_max) * live0
        w1 = jnp.exp(s1 - row_max) * live1
        total = jnp.sum(w0, axis=-1, keepdims=True) + jnp.sum(w1, axis=-1, keepdims=True)
        p0 = (w0 / total).astype(jnp.bfloat16)
        p1 = (w1 / total).astype(jnp.bfloat16)
        att = jnp.dot(p0, kv0_ref[0, :entry_len, vcols], preferred_element_type=jnp.float32)
        att = att + jnp.dot(p1, kv1_ref[0, :entry_len, vcols], preferred_element_type=jnp.float32)
        o_ref[:, cols] = att.astype(o_ref.dtype)


def attend(flat_idx, queries, slots, entry_len):
    tok_rows, head_cols = queries.shape
    segment_count = flat_idx.shape[0] // NBRS
    seg_rows = tok_rows // segment_count
    slot_rows, kv_cols = slots.shape[1], slots.shape[2]
    grid_spec = pltpu.PrefetchScalarGridSpec(
        num_scalar_prefetch=1,
        grid=(segment_count,),
        in_specs=[
            pl.BlockSpec((seg_rows, head_cols), lambda s, f: (s, 0)),
            pl.BlockSpec((1, slot_rows, kv_cols), lambda s, f: (f[s * NBRS], 0, 0)),
            pl.BlockSpec((1, slot_rows, kv_cols), lambda s, f: (f[s * NBRS + 1], 0, 0)),
        ],
        out_specs=pl.BlockSpec((seg_rows, head_cols), lambda s, f: (s, 0)),
    )
    return pl.pallas_call(
        functools.partial(attend_kernel, entry_len=entry_len),
        out_shape=jax.ShapeDtypeStruct((tok_rows, head_cols), jnp.bfloat16),
        grid_spec=grid_spec,
    )(flat_idx, queries, slots, slots)


def local(hidden_in, norm_gain, nbr_table, encodings, enc_mask, w_query, w_key, w_value, w_out):
    segment_count = nbr_table.shape[0]
    nb_dev, entry_len, enc_width = encodings.shape
    mask_cols = enc_mask.shape[1]
    head_cols = w_key.shape[1]
    wanted = nbr_table.reshape(-1)
    need_count = wanted.shape[0]

    gathered = lax.all_gather(hidden_in, "tensor", axis=1, tiled=True)

    w_both = jnp.concatenate([w_key, w_value], axis=1)
    own_kv = jnp.dot(
        encodings.reshape(nb_dev * entry_len, enc_width), w_both, preferred_element_type=jnp.float32
    ).astype(jnp.bfloat16).reshape(nb_dev, entry_len, 2 * head_cols)
    key_live = jnp.repeat(enc_mask, BLOCK, axis=1).astype(jnp.bfloat16)
    mask_rows = jnp.zeros((nb_dev, 8, 2 * head_cols), jnp.bfloat16)
    mask_rows = mask_rows.at[:, 0, :entry_len].set(key_live)
    own = jnp.concatenate([own_kv, mask_rows], axis=1)
    slots = lax.all_gather(own, "retr", axis=0, tiled=True)

    widened = gathered.astype(jnp.float32)
    mean_sq = jnp.mean(widened * widened, axis=-1, keepdims=True)
    normed = (widened * lax.rsqrt(mean_sq + 1e-05) * norm_gain).astype(jnp.bfloat16)
    queries = jnp.dot(normed, w_query, preferred_element_type=jnp.float32).astype(jnp.bfloat16)

    attended = attend(wanted, queries, slots, entry_len)
    partial_value = jnp.dot(attended, w_out, preferred_element_type=jnp.float32)
    summed = lax.psum_scatter(
        partial_value.astype(jnp.bfloat16), "tensor", scatter_dimension=1, tiled=True
    )
    return (hidden_in.astype(jnp.float32) + summed.astype(jnp.float32)).astype(jnp.bfloat16)


def solution(mesh):
    in_specs = (
        P(("dp", "retr"), "tensor"),
        P(),
        P(("dp", "retr"), None),
        P("retr", None, None),
        P("retr", None),
        P(None, "tensor"),
        P(None, "tensor"),
        P(None, "tensor"),
        P("tensor", None),
    )
    out_specs = P(("dp", "retr"), "tensor")
    return jax.shard_map(local, mesh=mesh, in_specs=in_specs, out_specs=out_specs, check_vma=False)
```

```python
import functools
import math

import jax
import jax.numpy as jnp
from jax import lax
from jax.experimental import pallas as pl
from jax.experimental.pallas import tpu as pltpu
from jax.sharding import PartitionSpec as P

HD = 128
NBRS = 2
BLOCK = 32
CAP = 2


def attend_kernel(flat_ref, q_ref, kv0_ref, kv1_ref, o_ref, *, entry_len):
    head_cols = q_ref.shape[1]
    factor = 1.0 / math.sqrt(HD)
    live0 = kv0_ref[0, entry_len:entry_len + 1, :entry_len].astype(jnp.float32)
    live1 = kv1_ref[0, entry_len:entry_len + 1, :entry_len].astype(jnp.float32)
    open0 = live0 > 0
    open1 = live1 > 0
    nt = (((1,), (1,)), ((), ()))
    for h in range(head_cols // HD):
        cols = slice(h * HD, (h + 1) * HD)
        vcols = slice(head_cols + h * HD, head_cols + (h + 1) * HD)
        qh = q_ref[:, cols]
        s0 = lax.dot_general(qh, kv0_ref[0, :entry_len, cols], nt, preferred_element_type=jnp.float32) * factor
        s1 = lax.dot_general(qh, kv1_ref[0, :entry_len, cols], nt, preferred_element_type=jnp.float32) * factor
        s0 = jnp.where(open0, s0, -1e30)
        s1 = jnp.where(open1, s1, -1e30)
        row_max = jnp.maximum(jnp.max(s0, axis=-1, keepdims=True), jnp.max(s1, axis=-1, keepdims=True))
        w0 = jnp.exp(s0 - row_max) * live0
        w1 = jnp.exp(s1 - row_max) * live1
        total = jnp.sum(w0, axis=-1, keepdims=True) + jnp.sum(w1, axis=-1, keepdims=True)
        p0 = (w0 / total).astype(jnp.bfloat16)
        p1 = (w1 / total).astype(jnp.bfloat16)
        att = jnp.dot(p0, kv0_ref[0, :entry_len, vcols], preferred_element_type=jnp.float32)
        att = att + jnp.dot(p1, kv1_ref[0, :entry_len, vcols], preferred_element_type=jnp.float32)
        o_ref[:, cols] = att.astype(o_ref.dtype)


def attend(flat_idx, queries, slots, entry_len):
    tok_rows, head_cols = queries.shape
    segment_count = flat_idx.shape[0] // NBRS
    seg_rows = tok_rows // segment_count
    slot_rows, kv_cols = slots.shape[1], slots.shape[2]
    grid_spec = pltpu.PrefetchScalarGridSpec(
        num_scalar_prefetch=1,
        grid=(segment_count,),
        in_specs=[
            pl.BlockSpec((seg_rows, head_cols), lambda s, f: (s, 0)),
            pl.BlockSpec((1, slot_rows, kv_cols), lambda s, f: (f[s * NBRS], 0, 0)),
            pl.BlockSpec((1, slot_rows, kv_cols), lambda s, f: (f[s * NBRS + 1], 0, 0)),
        ],
        out_specs=pl.BlockSpec((seg_rows, head_cols), lambda s, f: (s, 0)),
    )
    return pl.pallas_call(
        functools.partial(attend_kernel, entry_len=entry_len),
        out_shape=jax.ShapeDtypeStruct((tok_rows, head_cols), jnp.bfloat16),
        grid_spec=grid_spec,
    )(flat_idx, queries, slots, slots)


def local(hidden_in, norm_gain, nbr_table, encodings, enc_mask, w_query, w_key, w_value, w_out):
    segment_count = nbr_table.shape[0]
    nb_dev, entry_len, enc_width = encodings.shape
    mask_cols = enc_mask.shape[1]
    head_cols = w_key.shape[1]
    wanted = nbr_table.reshape(-1)
    need_count = wanted.shape[0]

    tensor_count = w_out.shape[1] // hidden_in.shape[1]
    feat = hidden_in.shape[1]
    t = lax.axis_index("tensor")
    pieces = [hidden_in]
    for k in range(1, tensor_count):
        perm = [(i, (i + k) % tensor_count) for i in range(tensor_count)]
        pieces.append(lax.ppermute(hidden_in, "tensor", perm))

    w_both = jnp.concatenate([w_key, w_value], axis=1)
    own_kv = jnp.dot(
        encodings.reshape(nb_dev * entry_len, enc_width), w_both, preferred_element_type=jnp.float32
    ).astype(jnp.bfloat16).reshape(nb_dev, entry_len, 2 * head_cols)
    key_live = jnp.repeat(enc_mask, BLOCK, axis=1).astype(jnp.bfloat16)
    mask_rows = jnp.zeros((nb_dev, 8, 2 * head_cols), jnp.bfloat16)
    mask_rows = mask_rows.at[:, 0, :entry_len].set(key_live)
    own = jnp.concatenate([own_kv, mask_rows], axis=1)
    slots = lax.all_gather(own, "retr", axis=0, tiled=True)

    widened = [p.astype(jnp.float32) for p in pieces]
    sum_sq = sum(jnp.sum(w * w, axis=-1, keepdims=True) for w in widened)
    inv = lax.rsqrt(sum_sq / (feat * tensor_count) + 1e-05)
    acc = None
    for k, w in enumerate(widened):
        src_block = (t - k) % tensor_count
        gain = lax.dynamic_slice_in_dim(norm_gain, src_block * feat, feat)
        normed = (w * inv * gain).astype(jnp.bfloat16)
        w_rows = lax.dynamic_slice_in_dim(w_query, src_block * feat, feat, axis=0)
        part = jnp.dot(normed, w_rows, preferred_element_type=jnp.float32)
        acc = part if acc is None else acc + part
    queries = acc.astype(jnp.bfloat16)

    attended = attend(wanted, queries, slots, entry_len)
    partial_value = jnp.dot(attended, w_out, preferred_element_type=jnp.float32)
    summed = lax.psum_scatter(
        partial_value.astype(jnp.bfloat16), "tensor", scatter_dimension=1, tiled=True
    )
    return (hidden_in.astype(jnp.float32) + summed.astype(jnp.float32)).astype(jnp.bfloat16)


def solution(mesh):
    in_specs = (
        P(("dp", "retr"), "tensor"),
        P(),
        P(("dp", "retr"), None),
        P("retr", None, None),
        P("retr", None),
        P(None, "tensor"),
        P(None, "tensor"),
        P(None, "tensor"),
        P("tensor", None),
    )
    out_specs = P(("dp", "retr"), "tensor")
    return jax.shard_map(local, mesh=mesh, in_specs=in_specs, out_specs=out_specs, check_vma=False)
```

```python
import functools
import math

import jax
import jax.numpy as jnp
from jax import lax
from jax.experimental import pallas as pl
from jax.experimental.pallas import tpu as pltpu
from jax.sharding import PartitionSpec as P

HD = 128
NBRS = 2
BLOCK = 32
CAP = 2


def attend_kernel(flat_ref, q_ref, kv0_ref, kv1_ref, o_ref, *, entry_len):
    head_cols = q_ref.shape[1]
    factor = 1.0 / math.sqrt(HD)
    live0 = kv0_ref[0, entry_len:entry_len + 1, :entry_len].astype(jnp.float32)
    live1 = kv1_ref[0, entry_len:entry_len + 1, :entry_len].astype(jnp.float32)
    open0 = live0 > 0
    open1 = live1 > 0
    nt = (((1,), (1,)), ((), ()))
    for h in range(head_cols // HD):
        cols = slice(h * HD, (h + 1) * HD)
        vcols = slice(head_cols + h * HD, head_cols + (h + 1) * HD)
        qh = q_ref[:, cols]
        s0 = lax.dot_general(qh, kv0_ref[0, :entry_len, cols], nt, preferred_element_type=jnp.float32) * factor
        s1 = lax.dot_general(qh, kv1_ref[0, :entry_len, cols], nt, preferred_element_type=jnp.float32) * factor
        s0 = jnp.where(open0, s0, -1e30)
        s1 = jnp.where(open1, s1, -1e30)
        row_max = jnp.maximum(jnp.max(s0, axis=-1, keepdims=True), jnp.max(s1, axis=-1, keepdims=True))
        w0 = jnp.exp(s0 - row_max) * live0
        w1 = jnp.exp(s1 - row_max) * live1
        total = jnp.sum(w0, axis=-1, keepdims=True) + jnp.sum(w1, axis=-1, keepdims=True)
        p0 = (w0 / total).astype(jnp.bfloat16)
        p1 = (w1 / total).astype(jnp.bfloat16)
        att = jnp.dot(p0, kv0_ref[0, :entry_len, vcols], preferred_element_type=jnp.float32)
        att = att + jnp.dot(p1, kv1_ref[0, :entry_len, vcols], preferred_element_type=jnp.float32)
        o_ref[:, cols] = att.astype(o_ref.dtype)


def attend(flat_idx, queries, slots, entry_len):
    tok_rows, head_cols = queries.shape
    segment_count = flat_idx.shape[0] // NBRS
    seg_rows = tok_rows // segment_count
    slot_rows, kv_cols = slots.shape[1], slots.shape[2]
    grid_spec = pltpu.PrefetchScalarGridSpec(
        num_scalar_prefetch=1,
        grid=(segment_count,),
        in_specs=[
            pl.BlockSpec((seg_rows, head_cols), lambda s, f: (s, 0)),
            pl.BlockSpec((1, slot_rows, kv_cols), lambda s, f: (f[s * NBRS], 0, 0)),
            pl.BlockSpec((1, slot_rows, kv_cols), lambda s, f: (f[s * NBRS + 1], 0, 0)),
        ],
        out_specs=pl.BlockSpec((seg_rows, head_cols), lambda s, f: (s, 0)),
    )
    return pl.pallas_call(
        functools.partial(attend_kernel, entry_len=entry_len),
        out_shape=jax.ShapeDtypeStruct((tok_rows, head_cols), jnp.bfloat16),
        grid_spec=grid_spec,
    )(flat_idx, queries, slots, slots)


def local(dp_count, retr_count, tensor_count, hidden_in, norm_gain, nbr_table, encodings, enc_mask, w_query, w_key, w_value, w_out):
    segment_count = nbr_table.shape[0]
    nb_dev, entry_len, enc_width = encodings.shape
    mask_cols = enc_mask.shape[1]
    head_cols = w_key.shape[1]
    wanted = nbr_table.reshape(-1)
    need_count = wanted.shape[0]

    feat = hidden_in.shape[1]
    t = lax.axis_index("tensor")
    fwd = [(i, (i + 1) % tensor_count) for i in range(tensor_count)]
    bwd = [(i, (i - 1) % tensor_count) for i in range(tensor_count)]
    pieces = [(0, hidden_in)]
    up = down = hidden_in
    half_ring = tensor_count // 2
    for k in range(1, half_ring):
        up = lax.ppermute(up, "tensor", fwd)
        down = lax.ppermute(down, "tensor", bwd)
        pieces.append((k, up))
        pieces.append((tensor_count - k, down))
    half_rows = hidden_in.shape[0] // 2
    top = lax.ppermute(up[:half_rows], "tensor", fwd)
    bottom = lax.ppermute(down[half_rows:], "tensor", bwd)
    pieces.append((half_ring, jnp.concatenate([top, bottom], axis=0)))

    per_dev = nb_dev // dp_count
    dp_idx = lax.axis_index("dp")
    enc_half = lax.dynamic_slice_in_dim(encodings, dp_idx * per_dev, per_dev, axis=0)
    mask_half = lax.dynamic_slice_in_dim(enc_mask, dp_idx * per_dev, per_dev, axis=0)
    w_both = jnp.concatenate([w_key, w_value], axis=1)
    own_kv = jnp.dot(
        enc_half.reshape(per_dev * entry_len, enc_width), w_both, preferred_element_type=jnp.float32
    ).astype(jnp.bfloat16).reshape(per_dev, entry_len, 2 * head_cols)
    key_live = jnp.repeat(mask_half, BLOCK, axis=1).astype(jnp.bfloat16)
    mask_rows = jnp.zeros((per_dev, 8, 2 * head_cols), jnp.bfloat16)
    mask_rows = mask_rows.at[:, 0, :entry_len].set(key_live)
    own = jnp.concatenate([own_kv, mask_rows], axis=1)
    slots = lax.all_gather(own, ("dp", "retr"), axis=0, tiled=True)
    in_dev = wanted % nb_dev
    slot_of = ((in_dev // per_dev) * retr_count + wanted // nb_dev) * per_dev + in_dev % per_dev

    widened = [p.astype(jnp.float32) for _, p in pieces]
    sum_sq = sum(jnp.sum(w * w, axis=-1, keepdims=True) for w in widened)
    inv = lax.rsqrt(sum_sq / (feat * tensor_count) + 1e-05)
    acc = None
    for (k, _), w in zip(pieces, widened):
        src_block = (t - k) % tensor_count
        gain = lax.dynamic_slice_in_dim(norm_gain, src_block * feat, feat)
        normed = (w * inv * gain).astype(jnp.bfloat16)
        w_rows = lax.dynamic_slice_in_dim(w_query, src_block * feat, feat, axis=0)
        part = jnp.dot(normed, w_rows, preferred_element_type=jnp.float32)
        acc = part if acc is None else acc + part
    queries = acc.astype(jnp.bfloat16)

    attended = attend(slot_of, queries, slots, entry_len)
    partial_value = jnp.dot(attended, w_out, preferred_element_type=jnp.float32)
    summed = lax.psum_scatter(
        partial_value.astype(jnp.bfloat16), "tensor", scatter_dimension=1, tiled=True
    )
    return (hidden_in.astype(jnp.float32) + summed.astype(jnp.float32)).astype(jnp.bfloat16)


def solution(mesh):
    in_specs = (
        P(("dp", "retr"), "tensor"),
        P(),
        P(("dp", "retr"), None),
        P("retr", None, None),
        P("retr", None),
        P(None, "tensor"),
        P(None, "tensor"),
        P(None, "tensor"),
        P("tensor", None),
    )
    out_specs = P(("dp", "retr"), "tensor")
    body = functools.partial(local, mesh.shape["dp"], mesh.shape["retr"], mesh.shape["tensor"])
    return jax.shard_map(body, mesh=mesh, in_specs=in_specs, out_specs=out_specs, check_vma=False)
```

```python
import functools
import math

import jax
import jax.numpy as jnp
from jax import lax
from jax.experimental import pallas as pl
from jax.experimental.pallas import tpu as pltpu
from jax.sharding import PartitionSpec as P

HD = 128
NBRS = 2
BLOCK = 32
CAP = 2


def attend_kernel(flat_ref, q_ref, kv0_ref, kv1_ref, o_ref, *, entry_len):
    head_cols = q_ref.shape[1]
    factor = 1.0 / math.sqrt(HD)
    live0 = kv0_ref[0, entry_len:entry_len + 1, :entry_len].astype(jnp.float32)
    live1 = kv1_ref[0, entry_len:entry_len + 1, :entry_len].astype(jnp.float32)
    open0 = live0 > 0
    open1 = live1 > 0
    nt = (((1,), (1,)), ((), ()))
    for h in range(head_cols // HD):
        cols = slice(h * HD, (h + 1) * HD)
        vcols = slice(head_cols + h * HD, head_cols + (h + 1) * HD)
        qh = q_ref[:, cols]
        s0 = lax.dot_general(qh, kv0_ref[0, :entry_len, cols], nt, preferred_element_type=jnp.float32) * factor
        s1 = lax.dot_general(qh, kv1_ref[0, :entry_len, cols], nt, preferred_element_type=jnp.float32) * factor
        s0 = jnp.where(open0, s0, -1e30)
        s1 = jnp.where(open1, s1, -1e30)
        row_max = jnp.maximum(jnp.max(s0, axis=-1, keepdims=True), jnp.max(s1, axis=-1, keepdims=True))
        w0 = jnp.exp(s0 - row_max) * live0
        w1 = jnp.exp(s1 - row_max) * live1
        total = jnp.sum(w0, axis=-1, keepdims=True) + jnp.sum(w1, axis=-1, keepdims=True)
        p0 = (w0 / total).astype(jnp.bfloat16)
        p1 = (w1 / total).astype(jnp.bfloat16)
        att = jnp.dot(p0, kv0_ref[0, :entry_len, vcols], preferred_element_type=jnp.float32)
        att = att + jnp.dot(p1, kv1_ref[0, :entry_len, vcols], preferred_element_type=jnp.float32)
        o_ref[:, cols] = att.astype(o_ref.dtype)


def attend(flat_idx, queries, slots, entry_len):
    tok_rows, head_cols = queries.shape
    segment_count = flat_idx.shape[0] // NBRS
    seg_rows = tok_rows // segment_count
    slot_rows, kv_cols = slots.shape[1], slots.shape[2]
    grid_spec = pltpu.PrefetchScalarGridSpec(
        num_scalar_prefetch=1,
        grid=(segment_count,),
        in_specs=[
            pl.BlockSpec((seg_rows, head_cols), lambda s, f: (s, 0)),
            pl.BlockSpec((1, slot_rows, kv_cols), lambda s, f: (f[s * NBRS], 0, 0)),
            pl.BlockSpec((1, slot_rows, kv_cols), lambda s, f: (f[s * NBRS + 1], 0, 0)),
        ],
        out_specs=pl.BlockSpec((seg_rows, head_cols), lambda s, f: (s, 0)),
    )
    return pl.pallas_call(
        functools.partial(attend_kernel, entry_len=entry_len),
        out_shape=jax.ShapeDtypeStruct((tok_rows, head_cols), jnp.bfloat16),
        grid_spec=grid_spec,
    )(flat_idx, queries, slots, slots)


def local(dp_count, retr_count, tensor_count, hidden_in, norm_gain, nbr_table, encodings, enc_mask, w_query, w_key, w_value, w_out):
    segment_count = nbr_table.shape[0]
    nb_dev, entry_len, enc_width = encodings.shape
    mask_cols = enc_mask.shape[1]
    head_cols = w_key.shape[1]
    wanted = nbr_table.reshape(-1)
    need_count = wanted.shape[0]

    feat = hidden_in.shape[1]
    t = lax.axis_index("tensor")
    fwd = [(i, (i + 1) % tensor_count) for i in range(tensor_count)]
    bwd = [(i, (i - 1) % tensor_count) for i in range(tensor_count)]
    pieces = [(0, hidden_in)]
    up = down = hidden_in
    half_ring = tensor_count // 2
    for k in range(1, half_ring):
        up = lax.ppermute(up, "tensor", fwd)
        down = lax.ppermute(down, "tensor", bwd)
        pieces.append((k, up))
        pieces.append((tensor_count - k, down))
    half_rows = hidden_in.shape[0] // 2
    top = lax.ppermute(up[:half_rows], "tensor", fwd)
    bottom = lax.ppermute(down[half_rows:], "tensor", bwd)
    pieces.append((half_ring, jnp.concatenate([top, bottom], axis=0)))

    half = t % 2
    half_len = entry_len // 2
    enc_rows = lax.dynamic_slice_in_dim(encodings, half * half_len, half_len, axis=1)
    key_live = jnp.repeat(enc_mask, BLOCK, axis=1).astype(jnp.bfloat16)
    mask_rows = jnp.zeros((nb_dev, 8, enc_width), jnp.bfloat16)
    mask_rows = mask_rows.at[:, 0, :entry_len].set(key_live)
    payload = jnp.concatenate([enc_rows, mask_rows], axis=1)
    all_enc = lax.all_gather(payload, "retr", axis=0, tiled=True)
    mine = jnp.take(all_enc, wanted, axis=0)
    mine_rows = mine[:, :half_len]
    pair = [(i, i ^ 1) for i in range(tensor_count)]
    other_rows = lax.ppermute(mine_rows, "tensor", pair)

    w_both = jnp.concatenate([w_key, w_value], axis=1)

    def project(rows):
        out = jnp.dot(
            rows.reshape(need_count * half_len, enc_width), w_both,
            preferred_element_type=jnp.float32,
        )
        return out.astype(jnp.bfloat16).reshape(need_count, half_len, 2 * head_cols)

    kv_mine = project(mine_rows)
    kv_other = project(other_rows)
    live_row = jnp.roll(mine[:, half_len, :entry_len], -half * half_len, axis=-1)
    live_rows = jnp.zeros((need_count, 8, 2 * head_cols), jnp.bfloat16)
    live_rows = live_rows.at[:, 0, :entry_len].set(live_row)
    slots = jnp.concatenate([kv_mine, kv_other, live_rows], axis=1)
    slot_of = jnp.arange(need_count, dtype=jnp.int32)

    widened = [p.astype(jnp.float32) for _, p in pieces]
    sum_sq = sum(jnp.sum(w * w, axis=-1, keepdims=True) for w in widened)
    inv = lax.rsqrt(sum_sq / (feat * tensor_count) + 1e-05)
    acc = None
    for (k, _), w in zip(pieces, widened):
        src_block = (t - k) % tensor_count
        gain = lax.dynamic_slice_in_dim(norm_gain, src_block * feat, feat)
        normed = (w * inv * gain).astype(jnp.bfloat16)
        w_rows = lax.dynamic_slice_in_dim(w_query, src_block * feat, feat, axis=0)
        part = jnp.dot(normed, w_rows, preferred_element_type=jnp.float32)
        acc = part if acc is None else acc + part
    queries = acc.astype(jnp.bfloat16)

    attended = attend(slot_of, queries, slots, entry_len)
    partial_value = jnp.dot(attended, w_out, preferred_element_type=jnp.float32)
    summed = lax.psum_scatter(
        partial_value.astype(jnp.bfloat16), "tensor", scatter_dimension=1, tiled=True
    )
    return (hidden_in.astype(jnp.float32) + summed.astype(jnp.float32)).astype(jnp.bfloat16)


def solution(mesh):
    in_specs = (
        P(("dp", "retr"), "tensor"),
        P(),
        P(("dp", "retr"), None),
        P("retr", None, None),
        P("retr", None),
        P(None, "tensor"),
        P(None, "tensor"),
        P(None, "tensor"),
        P("tensor", None),
    )
    out_specs = P(("dp", "retr"), "tensor")
    body = functools.partial(local, mesh.shape["dp"], mesh.shape["retr"], mesh.shape["tensor"])
    return jax.shard_map(body, mesh=mesh, in_specs=in_specs, out_specs=out_specs, check_vma=False)
```

```python
import functools
import math

import jax
import jax.numpy as jnp
from jax import lax
from jax.experimental import pallas as pl
from jax.experimental.pallas import tpu as pltpu
from jax.sharding import PartitionSpec as P

HD = 128
NBRS = 2
BLOCK = 32
CAP = 2
PAIR_CHUNKS = 4


def attend_kernel(q_ref, a_ref, b_ref, l_ref, o_ref):
    head_cols = q_ref.shape[1]
    half_len = a_ref.shape[1]
    factor = 1.0 / math.sqrt(HD)
    nt = (((1,), (1,)), ((), ()))
    lives = [l_ref[e, 0:1, :].astype(jnp.float32) for e in range(NBRS)]
    opens = [live > 0 for live in lives]
    for h in range(head_cols // HD):
        cols = slice(h * HD, (h + 1) * HD)
        vcols = slice(head_cols + h * HD, head_cols + (h + 1) * HD)
        qh = q_ref[:, cols]
        scores = []
        for e in range(NBRS):
            keys = jnp.concatenate([a_ref[e, :, cols], b_ref[e, :, cols]], axis=0)
            s = lax.dot_general(qh, keys, nt, preferred_element_type=jnp.float32) * factor
            scores.append(jnp.where(opens[e], s, -1e30))
        row_max = scores[0].max(axis=-1, keepdims=True)
        for s in scores[1:]:
            row_max = jnp.maximum(row_max, s.max(axis=-1, keepdims=True))
        weights = [jnp.exp(s - row_max) * live for s, live in zip(scores, lives)]
        total = sum(jnp.sum(w, axis=-1, keepdims=True) for w in weights)
        att = None
        for e, w in enumerate(weights):
            probs = (w / total).astype(jnp.bfloat16)
            values = jnp.concatenate([a_ref[e, :, vcols], b_ref[e, :, vcols]], axis=0)
            part = jnp.dot(probs, values, preferred_element_type=jnp.float32)
            att = part if att is None else att + part
        o_ref[:, cols] = att.astype(o_ref.dtype)


def attend(queries, kv_a, kv_b, live):
    tok_rows, head_cols = queries.shape
    segment_count = kv_a.shape[0] // NBRS
    seg_rows = tok_rows // segment_count
    half_len, kv_cols = kv_a.shape[1], kv_a.shape[2]
    live_rows, key_count = live.shape[1], live.shape[2]
    return pl.pallas_call(
        attend_kernel,
        out_shape=jax.ShapeDtypeStruct((tok_rows, head_cols), jnp.bfloat16),
        grid=(segment_count,),
        in_specs=[
            pl.BlockSpec((seg_rows, head_cols), lambda s: (s, 0)),
            pl.BlockSpec((NBRS, half_len, kv_cols), lambda s: (s, 0, 0)),
            pl.BlockSpec((NBRS, half_len, kv_cols), lambda s: (s, 0, 0)),
            pl.BlockSpec((NBRS, live_rows, key_count), lambda s: (s, 0, 0)),
        ],
        out_specs=pl.BlockSpec((seg_rows, head_cols), lambda s: (s, 0)),
    )(queries, kv_a, kv_b, live)


def local(dp_count, retr_count, tensor_count, hidden_in, norm_gain, nbr_table, encodings, enc_mask, w_query, w_key, w_value, w_out):
    segment_count = nbr_table.shape[0]
    nb_dev, entry_len, enc_width = encodings.shape
    mask_cols = enc_mask.shape[1]
    head_cols = w_key.shape[1]
    wanted = nbr_table.reshape(-1)
    need_count = wanted.shape[0]

    feat = hidden_in.shape[1]
    t = lax.axis_index("tensor")
    fwd = [(i, (i + 1) % tensor_count) for i in range(tensor_count)]
    bwd = [(i, (i - 1) % tensor_count) for i in range(tensor_count)]
    pieces = [(0, hidden_in)]
    up = down = hidden_in
    half_ring = tensor_count // 2
    for k in range(1, half_ring):
        up = lax.ppermute(up, "tensor", fwd)
        down = lax.ppermute(down, "tensor", bwd)
        pieces.append((k, up))
        pieces.append((tensor_count - k, down))
    half_rows = hidden_in.shape[0] // 2
    top = lax.ppermute(up[:half_rows], "tensor", fwd)
    bottom = lax.ppermute(down[half_rows:], "tensor", bwd)
    pieces.append((half_ring, jnp.concatenate([top, bottom], axis=0)))

    half = t % 2
    half_len = entry_len // 2
    enc_rows = lax.dynamic_slice_in_dim(encodings, half * half_len, half_len, axis=1)
    key_live = jnp.repeat(enc_mask, BLOCK, axis=1).astype(jnp.bfloat16)
    mask_rows = jnp.zeros((nb_dev, 8, enc_width), jnp.bfloat16)
    mask_rows = mask_rows.at[:, 0, :entry_len].set(key_live)
    payload = jnp.concatenate([enc_rows, mask_rows], axis=1)
    all_enc = lax.all_gather(payload, "retr", axis=0, tiled=True)
    mine = jnp.take(all_enc, wanted, axis=0)
    mine_rows = mine[:, :half_len]
    pair = [(i, i ^ 1) for i in range(tensor_count)]
    chunk = need_count // PAIR_CHUNKS
    other_chunks = [
        lax.ppermute(mine_rows[c * chunk:(c + 1) * chunk], "tensor", pair)
        for c in range(PAIR_CHUNKS)
    ]

    w_both = jnp.concatenate([w_key, w_value], axis=1)

    def project(rows):
        count = rows.shape[0]
        out = jnp.dot(
            rows.reshape(count * half_len, enc_width), w_both,
            preferred_element_type=jnp.float32,
        )
        return out.astype(jnp.bfloat16).reshape(count, half_len, 2 * head_cols)

    kv_mine = project(mine_rows)
    kv_other = jnp.concatenate([project(c) for c in other_chunks], axis=0)
    live_row = jnp.roll(mine[:, half_len:half_len + 8, :entry_len], -half * half_len, axis=-1)

    widened = [p.astype(jnp.float32) for _, p in pieces]
    sum_sq = sum(jnp.sum(w * w, axis=-1, keepdims=True) for w in widened)
    inv = lax.rsqrt(sum_sq / (feat * tensor_count) + 1e-05)
    acc = None
    for (k, _), w in zip(pieces, widened):
        src_block = (t - k) % tensor_count
        gain = lax.dynamic_slice_in_dim(norm_gain, src_block * feat, feat)
        normed = (w * inv * gain).astype(jnp.bfloat16)
        w_rows = lax.dynamic_slice_in_dim(w_query, src_block * feat, feat, axis=0)
        part = jnp.dot(normed, w_rows, preferred_element_type=jnp.float32)
        acc = part if acc is None else acc + part
    queries = acc.astype(jnp.bfloat16)

    attended = attend(queries, kv_mine, kv_other, live_row)
    partial_value = jnp.dot(attended, w_out, preferred_element_type=jnp.float32)
    summed = lax.psum_scatter(
        partial_value.astype(jnp.bfloat16), "tensor", scatter_dimension=1, tiled=True
    )
    return (hidden_in.astype(jnp.float32) + summed.astype(jnp.float32)).astype(jnp.bfloat16)


def solution(mesh):
    in_specs = (
        P(("dp", "retr"), "tensor"),
        P(),
        P(("dp", "retr"), None),
        P("retr", None, None),
        P("retr", None),
        P(None, "tensor"),
        P(None, "tensor"),
        P(None, "tensor"),
        P("tensor", None),
    )
    out_specs = P(("dp", "retr"), "tensor")
    body = functools.partial(local, mesh.shape["dp"], mesh.shape["retr"], mesh.shape["tensor"])
    return jax.shard_map(body, mesh=mesh, in_specs=in_specs, out_specs=out_specs, check_vma=False)
```

```python
import functools
import math

import jax
import jax.numpy as jnp
from jax import lax
from jax.experimental import pallas as pl
from jax.experimental.pallas import tpu as pltpu
from jax.sharding import PartitionSpec as P

HD = 128
NBRS = 2
BLOCK = 32
CAP = 2


def attend_kernel(q_ref, a_ref, b_ref, l_ref, o_ref):
    head_cols = q_ref.shape[1]
    half_len = a_ref.shape[1]
    factor = 1.0 / math.sqrt(HD)
    nt = (((1,), (1,)), ((), ()))
    lives = [l_ref[e, 0:1, :].astype(jnp.float32) for e in range(NBRS)]
    opens = [live > 0 for live in lives]
    for h in range(head_cols // HD):
        cols = slice(h * HD, (h + 1) * HD)
        vcols = slice(head_cols + h * HD, head_cols + (h + 1) * HD)
        qh = q_ref[:, cols]
        scores = []
        for e in range(NBRS):
            keys = jnp.concatenate([a_ref[e, :, cols], b_ref[e, :, cols]], axis=0)
            s = lax.dot_general(qh, keys, nt, preferred_element_type=jnp.float32) * factor
            scores.append(jnp.where(opens[e], s, -1e30))
        row_max = scores[0].max(axis=-1, keepdims=True)
        for s in scores[1:]:
            row_max = jnp.maximum(row_max, s.max(axis=-1, keepdims=True))
        weights = [jnp.exp(s - row_max) * live for s, live in zip(scores, lives)]
        total = sum(jnp.sum(w, axis=-1, keepdims=True) for w in weights)
        att = None
        for e, w in enumerate(weights):
            probs = (w / total).astype(jnp.bfloat16)
            values = jnp.concatenate([a_ref[e, :, vcols], b_ref[e, :, vcols]], axis=0)
            part = jnp.dot(probs, values, preferred_element_type=jnp.float32)
            att = part if att is None else att + part
        o_ref[:, cols] = att.astype(o_ref.dtype)


def attend(queries, kv_a, kv_b, live):
    tok_rows, head_cols = queries.shape
    segment_count = kv_a.shape[0] // NBRS
    seg_rows = tok_rows // segment_count
    half_len, kv_cols = kv_a.shape[1], kv_a.shape[2]
    live_rows, key_count = live.shape[1], live.shape[2]
    return pl.pallas_call(
        attend_kernel,
        out_shape=jax.ShapeDtypeStruct((tok_rows, head_cols), jnp.bfloat16),
        grid=(segment_count,),
        in_specs=[
            pl.BlockSpec((seg_rows, head_cols), lambda s: (s, 0)),
            pl.BlockSpec((NBRS, half_len, kv_cols), lambda s: (s, 0, 0)),
            pl.BlockSpec((NBRS, half_len, kv_cols), lambda s: (s, 0, 0)),
            pl.BlockSpec((NBRS, live_rows, key_count), lambda s: (s, 0, 0)),
        ],
        out_specs=pl.BlockSpec((seg_rows, head_cols), lambda s: (s, 0)),
    )(queries, kv_a, kv_b, live)


def local(dp_count, retr_count, tensor_count, hidden_in, norm_gain, nbr_table, encodings, enc_mask, w_query, w_key, w_value, w_out):
    segment_count = nbr_table.shape[0]
    nb_dev, entry_len, enc_width = encodings.shape
    mask_cols = enc_mask.shape[1]
    head_cols = w_key.shape[1]
    wanted = nbr_table.reshape(-1)
    need_count = wanted.shape[0]

    feat = hidden_in.shape[1]
    t = lax.axis_index("tensor")
    fwd = [(i, (i + 1) % tensor_count) for i in range(tensor_count)]
    bwd = [(i, (i - 1) % tensor_count) for i in range(tensor_count)]
    pieces = [(0, hidden_in)]
    up = down = hidden_in
    half_ring = tensor_count // 2
    for k in range(1, half_ring):
        up = lax.ppermute(up, "tensor", fwd)
        down = lax.ppermute(down, "tensor", bwd)
        pieces.append((k, up))
        pieces.append((tensor_count - k, down))
    half_rows = hidden_in.shape[0] // 2
    top = lax.ppermute(up[:half_rows], "tensor", fwd)
    bottom = lax.ppermute(down[half_rows:], "tensor", bwd)
    pieces.append((half_ring, jnp.concatenate([top, bottom], axis=0)))

    half = t % 2
    half_len = entry_len // 2
    part_len = half_len // 2
    key_live = jnp.repeat(enc_mask, BLOCK, axis=1).astype(jnp.bfloat16)
    mask_rows = jnp.zeros((nb_dev, 8, enc_width), jnp.bfloat16)
    mask_rows = mask_rows.at[:, 0, :entry_len].set(key_live)
    pair = [(i, i ^ 1) for i in range(tensor_count)]
    own_parts, other_parts = [], []
    live_row = None
    for p in range(2):
        rows = lax.dynamic_slice_in_dim(
            encodings, half * half_len + p * part_len, part_len, axis=1
        )
        if p == 0:
            rows = jnp.concatenate([rows, mask_rows], axis=1)
        gathered_rows = lax.all_gather(rows, "retr", axis=0, tiled=True)
        mine = jnp.take(gathered_rows, wanted, axis=0)
        if p == 0:
            live_row = jnp.roll(
                mine[:, part_len:part_len + 8, :entry_len], -half * half_len, axis=-1
            )
        mine_rows = mine[:, :part_len]
        own_parts.append(mine_rows)
        other_parts.append(lax.ppermute(mine_rows, "tensor", pair))

    w_both = jnp.concatenate([w_key, w_value], axis=1)

    def project(rows):
        count = rows.shape[0]
        out = jnp.dot(
            rows.reshape(count * half_len, enc_width), w_both,
            preferred_element_type=jnp.float32,
        )
        return out.astype(jnp.bfloat16).reshape(count, half_len, 2 * head_cols)

    kv_mine = project(jnp.concatenate(own_parts, axis=1))
    kv_other = project(jnp.concatenate(other_parts, axis=1))

    widened = [p.astype(jnp.float32) for _, p in pieces]
    sum_sq = sum(jnp.sum(w * w, axis=-1, keepdims=True) for w in widened)
    inv = lax.rsqrt(sum_sq / (feat * tensor_count) + 1e-05)
    acc = None
    for (k, _), w in zip(pieces, widened):
        src_block = (t - k) % tensor_count
        gain = lax.dynamic_slice_in_dim(norm_gain, src_block * feat, feat)
        normed = (w * inv * gain).astype(jnp.bfloat16)
        w_rows = lax.dynamic_slice_in_dim(w_query, src_block * feat, feat, axis=0)
        part = jnp.dot(normed, w_rows, preferred_element_type=jnp.float32)
        acc = part if acc is None else acc + part
    queries = acc.astype(jnp.bfloat16)

    attended = attend(queries, kv_mine, kv_other, live_row)
    partial_value = jnp.dot(attended, w_out, preferred_element_type=jnp.float32)
    summed = lax.psum_scatter(
        partial_value.astype(jnp.bfloat16), "tensor", scatter_dimension=1, tiled=True
    )
    return (hidden_in.astype(jnp.float32) + summed.astype(jnp.float32)).astype(jnp.bfloat16)


def solution(mesh):
    in_specs = (
        P(("dp", "retr"), "tensor"),
        P(),
        P(("dp", "retr"), None),
        P("retr", None, None),
        P("retr", None),
        P(None, "tensor"),
        P(None, "tensor"),
        P(None, "tensor"),
        P("tensor", None),
    )
    out_specs = P(("dp", "retr"), "tensor")
    body = functools.partial(local, mesh.shape["dp"], mesh.shape["retr"], mesh.shape["tensor"])
    return jax.shard_map(body, mesh=mesh, in_specs=in_specs, out_specs=out_specs, check_vma=False)
```

```python
import functools
import math

import jax
import jax.numpy as jnp
from jax import lax
from jax.experimental import pallas as pl
from jax.experimental.pallas import tpu as pltpu
from jax.sharding import PartitionSpec as P

HD = 128
NBRS = 2
BLOCK = 32
CAP = 2
OUT_CHUNKS = 2


def attend_kernel(flat_ref, q_ref, kv0_ref, kv1_ref, o_ref, *, entry_len):
    head_cols = q_ref.shape[1]
    factor = 1.0 / math.sqrt(HD)
    live0 = kv0_ref[0, entry_len:entry_len + 1, :entry_len].astype(jnp.float32)
    live1 = kv1_ref[0, entry_len:entry_len + 1, :entry_len].astype(jnp.float32)
    open0 = live0 > 0
    open1 = live1 > 0
    nt = (((1,), (1,)), ((), ()))
    for h in range(head_cols // HD):
        cols = slice(h * HD, (h + 1) * HD)
        vcols = slice(head_cols + h * HD, head_cols + (h + 1) * HD)
        qh = q_ref[:, cols]
        s0 = lax.dot_general(qh, kv0_ref[0, :entry_len, cols], nt, preferred_element_type=jnp.float32) * factor
        s1 = lax.dot_general(qh, kv1_ref[0, :entry_len, cols], nt, preferred_element_type=jnp.float32) * factor
        s0 = jnp.where(open0, s0, -1e30)
        s1 = jnp.where(open1, s1, -1e30)
        row_max = jnp.maximum(jnp.max(s0, axis=-1, keepdims=True), jnp.max(s1, axis=-1, keepdims=True))
        w0 = jnp.exp(s0 - row_max) * live0
        w1 = jnp.exp(s1 - row_max) * live1
        total = jnp.sum(w0, axis=-1, keepdims=True) + jnp.sum(w1, axis=-1, keepdims=True)
        p0 = (w0 / total).astype(jnp.bfloat16)
        p1 = (w1 / total).astype(jnp.bfloat16)
        att = jnp.dot(p0, kv0_ref[0, :entry_len, vcols], preferred_element_type=jnp.float32)
        att = att + jnp.dot(p1, kv1_ref[0, :entry_len, vcols], preferred_element_type=jnp.float32)
        o_ref[:, cols] = att.astype(o_ref.dtype)


def attend(flat_idx, queries, slots, entry_len):
    tok_rows, head_cols = queries.shape
    segment_count = flat_idx.shape[0] // NBRS
    seg_rows = tok_rows // segment_count
    slot_rows, kv_cols = slots.shape[1], slots.shape[2]
    grid_spec = pltpu.PrefetchScalarGridSpec(
        num_scalar_prefetch=1,
        grid=(segment_count,),
        in_specs=[
            pl.BlockSpec((seg_rows, head_cols), lambda s, f: (s, 0)),
            pl.BlockSpec((1, slot_rows, kv_cols), lambda s, f: (f[s * NBRS], 0, 0)),
            pl.BlockSpec((1, slot_rows, kv_cols), lambda s, f: (f[s * NBRS + 1], 0, 0)),
        ],
        out_specs=pl.BlockSpec((seg_rows, head_cols), lambda s, f: (s, 0)),
    )
    return pl.pallas_call(
        functools.partial(attend_kernel, entry_len=entry_len),
        out_shape=jax.ShapeDtypeStruct((tok_rows, head_cols), jnp.bfloat16),
        grid_spec=grid_spec,
    )(flat_idx, queries, slots, slots)


def local(dp_count, retr_count, tensor_count, hidden_in, norm_gain, nbr_table, encodings, enc_mask, w_query, w_key, w_value, w_out):
    segment_count = nbr_table.shape[0]
    nb_dev, entry_len, enc_width = encodings.shape
    mask_cols = enc_mask.shape[1]
    head_cols = w_key.shape[1]
    wanted = nbr_table.reshape(-1)
    need_count = wanted.shape[0]

    feat = hidden_in.shape[1]
    t = lax.axis_index("tensor")
    fwd = [(i, (i + 1) % tensor_count) for i in range(tensor_count)]
    bwd = [(i, (i - 1) % tensor_count) for i in range(tensor_count)]
    pieces = [(0, hidden_in)]
    up = down = hidden_in
    half_ring = tensor_count // 2
    for k in range(1, half_ring):
        up = lax.ppermute(up, "tensor", fwd)
        down = lax.ppermute(down, "tensor", bwd)
        pieces.append((k, up))
        pieces.append((tensor_count - k, down))
    half_rows = hidden_in.shape[0] // 2
    top = lax.ppermute(up[:half_rows], "tensor", fwd)
    bottom = lax.ppermute(down[half_rows:], "tensor", bwd)
    pieces.append((half_ring, jnp.concatenate([top, bottom], axis=0)))

    per_dev = nb_dev // dp_count
    dp_idx = lax.axis_index("dp")
    enc_half = lax.dynamic_slice_in_dim(encodings, dp_idx * per_dev, per_dev, axis=0)
    mask_half = lax.dynamic_slice_in_dim(enc_mask, dp_idx * per_dev, per_dev, axis=0)
    w_both = jnp.concatenate([w_key, w_value], axis=1)
    own_kv = jnp.dot(
        enc_half.reshape(per_dev * entry_len, enc_width), w_both, preferred_element_type=jnp.float32
    ).astype(jnp.bfloat16).reshape(per_dev, entry_len, 2 * head_cols)
    key_live = jnp.repeat(mask_half, BLOCK, axis=1).astype(jnp.bfloat16)
    mask_rows = jnp.zeros((per_dev, 8, 2 * head_cols), jnp.bfloat16)
    mask_rows = mask_rows.at[:, 0, :entry_len].set(key_live)
    own = jnp.concatenate([own_kv, mask_rows], axis=1)
    slots = lax.all_gather(own, ("dp", "retr"), axis=0, tiled=True)
    in_dev = wanted % nb_dev
    slot_of = ((in_dev // per_dev) * retr_count + wanted // nb_dev) * per_dev + in_dev % per_dev

    widened = [p.astype(jnp.float32) for _, p in pieces]
    sum_sq = sum(jnp.sum(w * w, axis=-1, keepdims=True) for w in widened)
    inv = lax.rsqrt(sum_sq / (feat * tensor_count) + 1e-05)
    acc = None
    for (k, _), w in zip(pieces, widened):
        src_block = (t - k) % tensor_count
        gain = lax.dynamic_slice_in_dim(norm_gain, src_block * feat, feat)
        normed = (w * inv * gain).astype(jnp.bfloat16)
        w_rows = lax.dynamic_slice_in_dim(w_query, src_block * feat, feat, axis=0)
        part = jnp.dot(normed, w_rows, preferred_element_type=jnp.float32)
        acc = part if acc is None else acc + part
    queries = acc.astype(jnp.bfloat16)

    tok_rows = queries.shape[0]
    outs = []
    for c in range(OUT_CHUNKS):
        rows = slice(c * tok_rows // OUT_CHUNKS, (c + 1) * tok_rows // OUT_CHUNKS)
        ids = slice(c * need_count // OUT_CHUNKS, (c + 1) * need_count // OUT_CHUNKS)
        attended = attend(slot_of[ids], queries[rows], slots, entry_len)
        partial_value = jnp.dot(attended, w_out, preferred_element_type=jnp.float32)
        summed = lax.psum_scatter(
            partial_value.astype(jnp.bfloat16), "tensor", scatter_dimension=1, tiled=True
        )
        outs.append(
            (hidden_in[rows].astype(jnp.float32) + summed.astype(jnp.float32)).astype(jnp.bfloat16)
        )
    return jnp.concatenate(outs, axis=0)


def solution(mesh):
    in_specs = (
        P(("dp", "retr"), "tensor"),
        P(),
        P(("dp", "retr"), None),
        P("retr", None, None),
        P("retr", None),
        P(None, "tensor"),
        P(None, "tensor"),
        P(None, "tensor"),
        P("tensor", None),
    )
    out_specs = P(("dp", "retr"), "tensor")
    body = functools.partial(local, mesh.shape["dp"], mesh.shape["retr"], mesh.shape["tensor"])
    return jax.shard_map(body, mesh=mesh, in_specs=in_specs, out_specs=out_specs, check_vma=False)
```

```python
import functools
import math

import jax
import jax.numpy as jnp
from jax import lax
from jax.experimental import pallas as pl
from jax.experimental.pallas import tpu as pltpu
from jax.sharding import PartitionSpec as P

HD = 128
NBRS = 2
BLOCK = 32
CAP = 2


def attend_kernel(flat_ref, q_ref, kv0_ref, kv1_ref, o_ref, *, entry_len):
    head_cols = q_ref.shape[1]
    factor = 1.0 / math.sqrt(HD)
    live = jnp.concatenate(
        [
            kv0_ref[0, entry_len:entry_len + 1, :entry_len],
            kv1_ref[0, entry_len:entry_len + 1, :entry_len],
        ],
        axis=1,
    ).astype(jnp.float32)
    key_open = live > 0
    nt = (((1,), (1,)), ((), ()))
    for h in range(head_cols // HD):
        cols = slice(h * HD, (h + 1) * HD)
        vcols = slice(head_cols + h * HD, head_cols + (h + 1) * HD)
        keys = jnp.concatenate([kv0_ref[0, :entry_len, cols], kv1_ref[0, :entry_len, cols]], axis=0)
        values = jnp.concatenate(
            [kv0_ref[0, :entry_len, vcols], kv1_ref[0, :entry_len, vcols]], axis=0
        )
        scores = lax.dot_general(q_ref[:, cols], keys, nt, preferred_element_type=jnp.float32) * factor
        scores = jnp.where(key_open, scores, -1e30)
        row_max = jnp.max(scores, axis=-1, keepdims=True)
        weights = jnp.exp(scores - row_max) * live
        probs = (weights / jnp.sum(weights, axis=-1, keepdims=True)).astype(jnp.bfloat16)
        att = jnp.dot(probs, values, preferred_element_type=jnp.float32)
        o_ref[:, cols] = att.astype(o_ref.dtype)


def attend(flat_idx, queries, slots, entry_len):
    tok_rows, head_cols = queries.shape
    segment_count = flat_idx.shape[0] // NBRS
    seg_rows = tok_rows // segment_count
    slot_rows, kv_cols = slots.shape[1], slots.shape[2]
    grid_spec = pltpu.PrefetchScalarGridSpec(
        num_scalar_prefetch=1,
        grid=(segment_count,),
        in_specs=[
            pl.BlockSpec((seg_rows, head_cols), lambda s, f: (s, 0)),
            pl.BlockSpec((1, slot_rows, kv_cols), lambda s, f: (f[s * NBRS], 0, 0)),
            pl.BlockSpec((1, slot_rows, kv_cols), lambda s, f: (f[s * NBRS + 1], 0, 0)),
        ],
        out_specs=pl.BlockSpec((seg_rows, head_cols), lambda s, f: (s, 0)),
    )
    return pl.pallas_call(
        functools.partial(attend_kernel, entry_len=entry_len),
        out_shape=jax.ShapeDtypeStruct((tok_rows, head_cols), jnp.bfloat16),
        grid_spec=grid_spec,
    )(flat_idx, queries, slots, slots)


def local(dp_count, retr_count, tensor_count, hidden_in, norm_gain, nbr_table, encodings, enc_mask, w_query, w_key, w_value, w_out):
    segment_count = nbr_table.shape[0]
    nb_dev, entry_len, enc_width = encodings.shape
    mask_cols = enc_mask.shape[1]
    head_cols = w_key.shape[1]
    wanted = nbr_table.reshape(-1)
    need_count = wanted.shape[0]

    feat = hidden_in.shape[1]
    t = lax.axis_index("tensor")
    fwd = [(i, (i + 1) % tensor_count) for i in range(tensor_count)]
    bwd = [(i, (i - 1) % tensor_count) for i in range(tensor_count)]
    pieces = [(0, hidden_in)]
    up = down = hidden_in
    half_ring = tensor_count // 2
    for k in range(1, half_ring):
        up = lax.ppermute(up, "tensor", fwd)
        down = lax.ppermute(down, "tensor", bwd)
        pieces.append((k, up))
        pieces.append((tensor_count - k, down))
    half_rows = hidden_in.shape[0] // 2
    top = lax.ppermute(up[:half_rows], "tensor", fwd)
    bottom = lax.ppermute(down[half_rows:], "tensor", bwd)
    pieces.append((half_ring, jnp.concatenate([top, bottom], axis=0)))

    per_dev = nb_dev // dp_count
    dp_idx = lax.axis_index("dp")
    enc_half = lax.dynamic_slice_in_dim(encodings, dp_idx * per_dev, per_dev, axis=0)
    mask_half = lax.dynamic_slice_in_dim(enc_mask, dp_idx * per_dev, per_dev, axis=0)
    w_both = jnp.concatenate([w_key, w_value], axis=1)
    own_kv = jnp.dot(
        enc_half.reshape(per_dev * entry_len, enc_width), w_both, preferred_element_type=jnp.float32
    ).astype(jnp.bfloat16).reshape(per_dev, entry_len, 2 * head_cols)
    key_live = jnp.repeat(mask_half, BLOCK, axis=1).astype(jnp.bfloat16)
    mask_rows = jnp.zeros((per_dev, 8, 2 * head_cols), jnp.bfloat16)
    mask_rows = mask_rows.at[:, 0, :entry_len].set(key_live)
    own = jnp.concatenate([own_kv, mask_rows], axis=1)
    slots = lax.all_gather(own, ("dp", "retr"), axis=0, tiled=True)
    in_dev = wanted % nb_dev
    slot_of = ((in_dev // per_dev) * retr_count + wanted // nb_dev) * per_dev + in_dev % per_dev

    widened = [p.astype(jnp.float32) for _, p in pieces]
    sum_sq = sum(jnp.sum(w * w, axis=-1, keepdims=True) for w in widened)
    inv = lax.rsqrt(sum_sq / (feat * tensor_count) + 1e-05)
    acc = None
    for (k, _), w in zip(pieces, widened):
        src_block = (t - k) % tensor_count
        gain = lax.dynamic_slice_in_dim(norm_gain, src_block * feat, feat)
        normed = (w * inv * gain).astype(jnp.bfloat16)
        w_rows = lax.dynamic_slice_in_dim(w_query, src_block * feat, feat, axis=0)
        part = jnp.dot(normed, w_rows, preferred_element_type=jnp.float32)
        acc = part if acc is None else acc + part
    queries = acc.astype(jnp.bfloat16)

    attended = attend(slot_of, queries, slots, entry_len)
    partial_value = jnp.dot(attended, w_out, preferred_element_type=jnp.float32)
    summed = lax.psum_scatter(
        partial_value.astype(jnp.bfloat16), "tensor", scatter_dimension=1, tiled=True
    )
    return (hidden_in.astype(jnp.float32) + summed.astype(jnp.float32)).astype(jnp.bfloat16)


def solution(mesh):
    in_specs = (
        P(("dp", "retr"), "tensor"),
        P(),
        P(("dp", "retr"), None),
        P("retr", None, None),
        P("retr", None),
        P(None, "tensor"),
        P(None, "tensor"),
        P(None, "tensor"),
        P("tensor", None),
    )
    out_specs = P(("dp", "retr"), "tensor")
    body = functools.partial(local, mesh.shape["dp"], mesh.shape["retr"], mesh.shape["tensor"])
    return jax.shard_map(body, mesh=mesh, in_specs=in_specs, out_specs=out_specs, check_vma=False)
```

```python
import functools
import math

import jax
import jax.numpy as jnp
from jax import lax
from jax.experimental import pallas as pl
from jax.experimental.pallas import tpu as pltpu
from jax.sharding import PartitionSpec as P

HD = 128
NBRS = 2
BLOCK = 32
CAP = 2


def attend_kernel(flat_ref, q_ref, kv0_ref, kv1_ref, o_ref, *, entry_len):
    head_cols = q_ref.shape[1]
    factor = 1.0 / math.sqrt(HD)
    live = jnp.concatenate(
        [
            kv0_ref[0, entry_len:entry_len + 1, :entry_len],
            kv1_ref[0, entry_len:entry_len + 1, :entry_len],
        ],
        axis=1,
    ).astype(jnp.float32)
    key_open = live > 0
    for h in range(head_cols // HD):
        cols = slice(h * HD, (h + 1) * HD)
        vcols = slice(head_cols + h * HD, head_cols + (h + 1) * HD)
        kcols = slice(h * entry_len, (h + 1) * entry_len)
        keys_t = jnp.concatenate([kv0_ref[0, :HD, kcols], kv1_ref[0, :HD, kcols]], axis=1)
        values = jnp.concatenate(
            [kv0_ref[0, :entry_len, vcols], kv1_ref[0, :entry_len, vcols]], axis=0
        )
        scores = jnp.dot(q_ref[:, cols], keys_t, preferred_element_type=jnp.float32) * factor
        scores = jnp.where(key_open, scores, -1e30)
        row_max = jnp.max(scores, axis=-1, keepdims=True)
        weights = jnp.exp(scores - row_max) * live
        probs = (weights / jnp.sum(weights, axis=-1, keepdims=True)).astype(jnp.bfloat16)
        att = jnp.dot(probs, values, preferred_element_type=jnp.float32)
        o_ref[:, cols] = att.astype(o_ref.dtype)


def attend(flat_idx, queries, slots, entry_len):
    tok_rows, head_cols = queries.shape
    segment_count = flat_idx.shape[0] // NBRS
    seg_rows = tok_rows // segment_count
    slot_rows, kv_cols = slots.shape[1], slots.shape[2]
    grid_spec = pltpu.PrefetchScalarGridSpec(
        num_scalar_prefetch=1,
        grid=(segment_count,),
        in_specs=[
            pl.BlockSpec((seg_rows, head_cols), lambda s, f: (s, 0)),
            pl.BlockSpec((1, slot_rows, kv_cols), lambda s, f: (f[s * NBRS], 0, 0)),
            pl.BlockSpec((1, slot_rows, kv_cols), lambda s, f: (f[s * NBRS + 1], 0, 0)),
        ],
        out_specs=pl.BlockSpec((seg_rows, head_cols), lambda s, f: (s, 0)),
    )
    return pl.pallas_call(
        functools.partial(attend_kernel, entry_len=entry_len),
        out_shape=jax.ShapeDtypeStruct((tok_rows, head_cols), jnp.bfloat16),
        grid_spec=grid_spec,
    )(flat_idx, queries, slots, slots)


def local(dp_count, retr_count, tensor_count, hidden_in, norm_gain, nbr_table, encodings, enc_mask, w_query, w_key, w_value, w_out):
    segment_count = nbr_table.shape[0]
    nb_dev, entry_len, enc_width = encodings.shape
    mask_cols = enc_mask.shape[1]
    head_cols = w_key.shape[1]
    wanted = nbr_table.reshape(-1)
    need_count = wanted.shape[0]

    feat = hidden_in.shape[1]
    t = lax.axis_index("tensor")
    fwd = [(i, (i + 1) % tensor_count) for i in range(tensor_count)]
    bwd = [(i, (i - 1) % tensor_count) for i in range(tensor_count)]
    pieces = [(0, hidden_in)]
    up = down = hidden_in
    half_ring = tensor_count // 2
    for k in range(1, half_ring):
        up = lax.ppermute(up, "tensor", fwd)
        down = lax.ppermute(down, "tensor", bwd)
        pieces.append((k, up))
        pieces.append((tensor_count - k, down))
    half_rows = hidden_in.shape[0] // 2
    top = lax.ppermute(up[:half_rows], "tensor", fwd)
    bottom = lax.ppermute(down[half_rows:], "tensor", bwd)
    pieces.append((half_ring, jnp.concatenate([top, bottom], axis=0)))

    per_dev = nb_dev // dp_count
    dp_idx = lax.axis_index("dp")
    enc_half = lax.dynamic_slice_in_dim(encodings, dp_idx * per_dev, per_dev, axis=0)
    mask_half = lax.dynamic_slice_in_dim(enc_mask, dp_idx * per_dev, per_dev, axis=0)
    w_both = jnp.concatenate([w_key, w_value], axis=1)
    own_kv = jnp.dot(
        enc_half.reshape(per_dev * entry_len, enc_width), w_both, preferred_element_type=jnp.float32
    ).astype(jnp.bfloat16).reshape(per_dev, entry_len, 2 * head_cols)
    head_count = head_cols // HD
    keys_t = own_kv[:, :, :head_cols].reshape(per_dev, entry_len, head_count, HD)
    keys_t = keys_t.transpose(0, 3, 2, 1).reshape(per_dev, HD, head_count * entry_len)
    own_kv = jnp.concatenate([keys_t, own_kv[:, :, head_cols:]], axis=2)
    key_live = jnp.repeat(mask_half, BLOCK, axis=1).astype(jnp.bfloat16)
    mask_rows = jnp.zeros((per_dev, 8, 2 * head_cols), jnp.bfloat16)
    mask_rows = mask_rows.at[:, 0, :entry_len].set(key_live)
    own = jnp.concatenate([own_kv, mask_rows], axis=1)
    slots = lax.all_gather(own, ("dp", "retr"), axis=0, tiled=True)
    in_dev = wanted % nb_dev
    slot_of = ((in_dev // per_dev) * retr_count + wanted // nb_dev) * per_dev + in_dev % per_dev

    widened = [p.astype(jnp.float32) for _, p in pieces]
    sum_sq = sum(jnp.sum(w * w, axis=-1, keepdims=True) for w in widened)
    inv = lax.rsqrt(sum_sq / (feat * tensor_count) + 1e-05)
    acc = None
    for (k, _), w in zip(pieces, widened):
        src_block = (t - k) % tensor_count
        gain = lax.dynamic_slice_in_dim(norm_gain, src_block * feat, feat)
        normed = (w * inv * gain).astype(jnp.bfloat16)
        w_rows = lax.dynamic_slice_in_dim(w_query, src_block * feat, feat, axis=0)
        part = jnp.dot(normed, w_rows, preferred_element_type=jnp.float32)
        acc = part if acc is None else acc + part
    queries = acc.astype(jnp.bfloat16)

    attended = attend(slot_of, queries, slots, entry_len)
    partial_value = jnp.dot(attended, w_out, preferred_element_type=jnp.float32)
    summed = lax.psum_scatter(
        partial_value.astype(jnp.bfloat16), "tensor", scatter_dimension=1, tiled=True
    )
    return (hidden_in.astype(jnp.float32) + summed.astype(jnp.float32)).astype(jnp.bfloat16)


def solution(mesh):
    in_specs = (
        P(("dp", "retr"), "tensor"),
        P(),
        P(("dp", "retr"), None),
        P("retr", None, None),
        P("retr", None),
        P(None, "tensor"),
        P(None, "tensor"),
        P(None, "tensor"),
        P("tensor", None),
    )
    out_specs = P(("dp", "retr"), "tensor")
    body = functools.partial(local, mesh.shape["dp"], mesh.shape["retr"], mesh.shape["tensor"])
    return jax.shard_map(body, mesh=mesh, in_specs=in_specs, out_specs=out_specs, check_vma=False)
```

```python
import functools
import math

import jax
import jax.numpy as jnp
from jax import lax
from jax.experimental import pallas as pl
from jax.experimental.pallas import tpu as pltpu
from jax.sharding import PartitionSpec as P

HD = 128
NBRS = 2
BLOCK = 32
CAP = 2


def attend_kernel(flat_ref, q_ref, kv0_ref, kv1_ref, o_ref, *, entry_len):
    head_cols = q_ref.shape[1]
    factor = 1.0 / math.sqrt(HD)
    live = jnp.concatenate(
        [
            kv0_ref[0, entry_len:entry_len + 1, :entry_len],
            kv1_ref[0, entry_len:entry_len + 1, :entry_len],
        ],
        axis=1,
    ).astype(jnp.float32)
    key_open = live > 0
    for h in range(head_cols // HD):
        cols = slice(h * HD, (h + 1) * HD)
        vcols = slice(head_cols + h * HD, head_cols + (h + 1) * HD)
        kcols = slice(h * entry_len, (h + 1) * entry_len)
        keys_t = jnp.concatenate([kv0_ref[0, :HD, kcols], kv1_ref[0, :HD, kcols]], axis=1)
        values = jnp.concatenate(
            [kv0_ref[0, :entry_len, vcols], kv1_ref[0, :entry_len, vcols]], axis=0
        )
        scores = jnp.dot(q_ref[:, cols], keys_t, preferred_element_type=jnp.float32) * factor
        scores = jnp.where(key_open, scores, -1e30)
        row_max = jnp.max(scores, axis=-1, keepdims=True)
        weights = jnp.exp(scores - row_max) * live
        probs = (weights / jnp.sum(weights, axis=-1, keepdims=True)).astype(jnp.bfloat16)
        att = jnp.dot(probs, values, preferred_element_type=jnp.float32)
        o_ref[:, cols] = att.astype(o_ref.dtype)


def attend(flat_idx, queries, slots, entry_len):
    tok_rows, head_cols = queries.shape
    segment_count = flat_idx.shape[0] // NBRS
    seg_rows = tok_rows // segment_count
    slot_rows, kv_cols = slots.shape[1], slots.shape[2]
    grid_spec = pltpu.PrefetchScalarGridSpec(
        num_scalar_prefetch=1,
        grid=(segment_count,),
        in_specs=[
            pl.BlockSpec((seg_rows, head_cols), lambda s, f: (s, 0)),
            pl.BlockSpec((1, slot_rows, kv_cols), lambda s, f: (f[s * NBRS], 0, 0)),
            pl.BlockSpec((1, slot_rows, kv_cols), lambda s, f: (f[s * NBRS + 1], 0, 0)),
        ],
        out_specs=pl.BlockSpec((seg_rows, head_cols), lambda s, f: (s, 0)),
    )
    return pl.pallas_call(
        functools.partial(attend_kernel, entry_len=entry_len),
        out_shape=jax.ShapeDtypeStruct((tok_rows, head_cols), jnp.bfloat16),
        grid_spec=grid_spec,
    )(flat_idx, queries, slots, slots)


def local(dp_count, retr_count, tensor_count, hidden_in, norm_gain, nbr_table, encodings, enc_mask, w_query, w_key, w_value, w_out):
    segment_count = nbr_table.shape[0]
    nb_dev, entry_len, enc_width = encodings.shape
    mask_cols = enc_mask.shape[1]
    head_cols = w_key.shape[1]
    wanted = nbr_table.reshape(-1)
    need_count = wanted.shape[0]

    feat = hidden_in.shape[1]
    t = lax.axis_index("tensor")
    fwd = [(i, (i + 1) % tensor_count) for i in range(tensor_count)]
    bwd = [(i, (i - 1) % tensor_count) for i in range(tensor_count)]
    pieces = [(0, hidden_in)]
    up = down = hidden_in
    half_ring = tensor_count // 2
    for k in range(1, half_ring):
        up = lax.ppermute(up, "tensor", fwd)
        down = lax.ppermute(down, "tensor", bwd)
        pieces.append((k, up))
        pieces.append((tensor_count - k, down))
    half_rows = hidden_in.shape[0] // 2
    top = lax.ppermute(up[:half_rows], "tensor", fwd)
    bottom = lax.ppermute(down[half_rows:], "tensor", bwd)
    pieces.append((half_ring, jnp.concatenate([top, bottom], axis=0)))

    per_dev = nb_dev
    enc_half = encodings
    mask_half = enc_mask
    w_both = jnp.concatenate([w_key, w_value], axis=1)
    own_kv = jnp.dot(
        enc_half.reshape(per_dev * entry_len, enc_width), w_both, preferred_element_type=jnp.float32
    ).astype(jnp.bfloat16).reshape(per_dev, entry_len, 2 * head_cols)
    head_count = head_cols // HD
    keys_t = own_kv[:, :, :head_cols].reshape(per_dev, entry_len, head_count, HD)
    keys_t = keys_t.transpose(0, 3, 2, 1).reshape(per_dev, HD, head_count * entry_len)
    own_kv = jnp.concatenate([keys_t, own_kv[:, :, head_cols:]], axis=2)
    key_live = jnp.repeat(mask_half, BLOCK, axis=1).astype(jnp.bfloat16)
    mask_rows = jnp.zeros((per_dev, 8, 2 * head_cols), jnp.bfloat16)
    mask_rows = mask_rows.at[:, 0, :entry_len].set(key_live)
    own = jnp.concatenate([own_kv, mask_rows], axis=1)
    slots = lax.all_gather(own, "retr", axis=0, tiled=True)
    slot_of = wanted

    widened = [p.astype(jnp.float32) for _, p in pieces]
    sum_sq = sum(jnp.sum(w * w, axis=-1, keepdims=True) for w in widened)
    inv = lax.rsqrt(sum_sq / (feat * tensor_count) + 1e-05)
    acc = None
    for (k, _), w in zip(pieces, widened):
        src_block = (t - k) % tensor_count
        gain = lax.dynamic_slice_in_dim(norm_gain, src_block * feat, feat)
        normed = (w * inv * gain).astype(jnp.bfloat16)
        w_rows = lax.dynamic_slice_in_dim(w_query, src_block * feat, feat, axis=0)
        part = jnp.dot(normed, w_rows, preferred_element_type=jnp.float32)
        acc = part if acc is None else acc + part
    queries = acc.astype(jnp.bfloat16)

    attended = attend(slot_of, queries, slots, entry_len)
    partial_value = jnp.dot(attended, w_out, preferred_element_type=jnp.float32)
    summed = lax.psum_scatter(
        partial_value.astype(jnp.bfloat16), "tensor", scatter_dimension=1, tiled=True
    )
    return (hidden_in.astype(jnp.float32) + summed.astype(jnp.float32)).astype(jnp.bfloat16)


def solution(mesh):
    in_specs = (
        P(("dp", "retr"), "tensor"),
        P(),
        P(("dp", "retr"), None),
        P("retr", None, None),
        P("retr", None),
        P(None, "tensor"),
        P(None, "tensor"),
        P(None, "tensor"),
        P("tensor", None),
    )
    out_specs = P(("dp", "retr"), "tensor")
    body = functools.partial(local, mesh.shape["dp"], mesh.shape["retr"], mesh.shape["tensor"])
    return jax.shard_map(body, mesh=mesh, in_specs=in_specs, out_specs=out_specs, check_vma=False)
```

```python
import functools
import math

import jax
import jax.numpy as jnp
from jax import lax
from jax.experimental import pallas as pl
from jax.experimental.pallas import tpu as pltpu
from jax.sharding import PartitionSpec as P

HD = 128
NBRS = 2
BLOCK = 32
CAP = 2


def attend_kernel(flat_ref, q_ref, kv0_ref, kv1_ref, live_ref, o_ref, *, entry_len):
    head_cols = q_ref.shape[1]
    factor = 1.0 / math.sqrt(HD)
    live = live_ref[0]
    key_open = live > 0
    for h in range(head_cols // HD):
        cols = slice(h * HD, (h + 1) * HD)
        vcols = slice(head_cols + h * HD, head_cols + (h + 1) * HD)
        kcols = slice(h * entry_len, (h + 1) * entry_len)
        keys_t = jnp.concatenate([kv0_ref[0, :HD, kcols], kv1_ref[0, :HD, kcols]], axis=1)
        values = jnp.concatenate(
            [kv0_ref[0, :entry_len, vcols], kv1_ref[0, :entry_len, vcols]], axis=0
        )
        scores = jnp.dot(q_ref[:, cols], keys_t, preferred_element_type=jnp.float32) * factor
        scores = jnp.where(key_open, scores, -1e30)
        row_max = jnp.max(scores, axis=-1, keepdims=True)
        weights = jnp.exp(scores - row_max) * live
        probs = (weights / jnp.sum(weights, axis=-1, keepdims=True)).astype(jnp.bfloat16)
        att = jnp.dot(probs, values, preferred_element_type=jnp.float32)
        o_ref[:, cols] = att.astype(o_ref.dtype)


def attend(flat_idx, queries, slots, live, entry_len):
    tok_rows, head_cols = queries.shape
    segment_count = flat_idx.shape[0] // NBRS
    seg_rows = tok_rows // segment_count
    slot_rows, kv_cols = slots.shape[1], slots.shape[2]
    grid_spec = pltpu.PrefetchScalarGridSpec(
        num_scalar_prefetch=1,
        grid=(segment_count,),
        in_specs=[
            pl.BlockSpec((seg_rows, head_cols), lambda s, f: (s, 0)),
            pl.BlockSpec((1, slot_rows, kv_cols), lambda s, f: (f[s * NBRS], 0, 0)),
            pl.BlockSpec((1, slot_rows, kv_cols), lambda s, f: (f[s * NBRS + 1], 0, 0)),
            pl.BlockSpec((1, 1, live.shape[2]), lambda s, f: (s, 0, 0)),
        ],
        out_specs=pl.BlockSpec((seg_rows, head_cols), lambda s, f: (s, 0)),
    )
    return pl.pallas_call(
        functools.partial(attend_kernel, entry_len=entry_len),
        out_shape=jax.ShapeDtypeStruct((tok_rows, head_cols), jnp.bfloat16),
        grid_spec=grid_spec,
    )(flat_idx, queries, slots, slots, live)


def local(dp_count, retr_count, tensor_count, hidden_in, norm_gain, nbr_table, encodings, enc_mask, w_query, w_key, w_value, w_out):
    segment_count = nbr_table.shape[0]
    nb_dev, entry_len, enc_width = encodings.shape
    mask_cols = enc_mask.shape[1]
    head_cols = w_key.shape[1]
    wanted = nbr_table.reshape(-1)
    need_count = wanted.shape[0]

    feat = hidden_in.shape[1]
    t = lax.axis_index("tensor")
    fwd = [(i, (i + 1) % tensor_count) for i in range(tensor_count)]
    bwd = [(i, (i - 1) % tensor_count) for i in range(tensor_count)]
    pieces = [(0, hidden_in)]
    up = down = hidden_in
    half_ring = tensor_count // 2
    for k in range(1, half_ring):
        up = lax.ppermute(up, "tensor", fwd)
        down = lax.ppermute(down, "tensor", bwd)
        pieces.append((k, up))
        pieces.append((tensor_count - k, down))
    half_rows = hidden_in.shape[0] // 2
    top = lax.ppermute(up[:half_rows], "tensor", fwd)
    bottom = lax.ppermute(down[half_rows:], "tensor", bwd)
    pieces.append((half_ring, jnp.concatenate([top, bottom], axis=0)))

    per_dev = nb_dev
    enc_half = encodings
    mask_half = enc_mask
    w_both = jnp.concatenate([w_key, w_value], axis=1)
    own_kv = jnp.dot(
        enc_half.reshape(per_dev * entry_len, enc_width), w_both, preferred_element_type=jnp.float32
    ).astype(jnp.bfloat16).reshape(per_dev, entry_len, 2 * head_cols)
    head_count = head_cols // HD
    keys_t = own_kv[:, :, :head_cols].reshape(per_dev, entry_len, head_count, HD)
    keys_t = keys_t.transpose(0, 3, 2, 1).reshape(per_dev, HD, head_count * entry_len)
    own_kv = jnp.concatenate([keys_t, own_kv[:, :, head_cols:]], axis=2)
    slots = lax.all_gather(own_kv, "retr", axis=0, tiled=True)
    slot_of = wanted
    mask_copies = jnp.broadcast_to(mask_half[None], (retr_count,) + mask_half.shape)
    all_marks = lax.all_to_all(mask_copies, "retr", 0, 0, tiled=True)
    all_marks = all_marks.reshape(retr_count * nb_dev, mask_cols)
    key_live = jnp.repeat(jnp.take(all_marks, wanted, axis=0), BLOCK, axis=1)
    key_live = key_live.astype(jnp.float32).reshape(segment_count, 1, NBRS * entry_len)

    widened = [p.astype(jnp.float32) for _, p in pieces]
    sum_sq = sum(jnp.sum(w * w, axis=-1, keepdims=True) for w in widened)
    inv = lax.rsqrt(sum_sq / (feat * tensor_count) + 1e-05)
    acc = None
    for (k, _), w in zip(pieces, widened):
        src_block = (t - k) % tensor_count
        gain = lax.dynamic_slice_in_dim(norm_gain, src_block * feat, feat)
        normed = (w * inv * gain).astype(jnp.bfloat16)
        w_rows = lax.dynamic_slice_in_dim(w_query, src_block * feat, feat, axis=0)
        part = jnp.dot(normed, w_rows, preferred_element_type=jnp.float32)
        acc = part if acc is None else acc + part
    queries = acc.astype(jnp.bfloat16)

    attended = attend(slot_of, queries, slots, key_live, entry_len)
    partial_value = jnp.dot(attended, w_out, preferred_element_type=jnp.float32)
    summed = lax.psum_scatter(
        partial_value.astype(jnp.bfloat16), "tensor", scatter_dimension=1, tiled=True
    )
    return (hidden_in.astype(jnp.float32) + summed.astype(jnp.float32)).astype(jnp.bfloat16)


def solution(mesh):
    in_specs = (
        P(("dp", "retr"), "tensor"),
        P(),
        P(("dp", "retr"), None),
        P("retr", None, None),
        P("retr", None),
        P(None, "tensor"),
        P(None, "tensor"),
        P(None, "tensor"),
        P("tensor", None),
    )
    out_specs = P(("dp", "retr"), "tensor")
    body = functools.partial(local, mesh.shape["dp"], mesh.shape["retr"], mesh.shape["tensor"])
    return jax.shard_map(body, mesh=mesh, in_specs=in_specs, out_specs=out_specs, check_vma=False)
```

```python
import functools
import math

import jax
import jax.numpy as jnp
from jax import lax
from jax.experimental import pallas as pl
from jax.experimental.pallas import tpu as pltpu
from jax.sharding import PartitionSpec as P

HD = 128
NBRS = 2
BLOCK = 32
CAP = 2
SEGS_PER_STEP = 2


def attend_kernel(flat_ref, q_ref, *refs, entry_len):
    kv_refs, live_ref, o_ref = refs[:-2], refs[-2], refs[-1]
    head_cols = q_ref.shape[1]
    seg_rows = q_ref.shape[0] // SEGS_PER_STEP
    factor = 1.0 / math.sqrt(HD)
    for g in range(SEGS_PER_STEP):
        kv0_ref, kv1_ref = kv_refs[g * NBRS], kv_refs[g * NBRS + 1]
        rows = slice(g * seg_rows, (g + 1) * seg_rows)
        live = live_ref[g]
        key_open = live > 0
        for h in range(head_cols // HD):
            cols = slice(h * HD, (h + 1) * HD)
            vcols = slice(head_cols + h * HD, head_cols + (h + 1) * HD)
            kcols = slice(h * entry_len, (h + 1) * entry_len)
            keys_t = jnp.concatenate([kv0_ref[0, :HD, kcols], kv1_ref[0, :HD, kcols]], axis=1)
            values = jnp.concatenate(
                [kv0_ref[0, :entry_len, vcols], kv1_ref[0, :entry_len, vcols]], axis=0
            )
            scores = jnp.dot(q_ref[rows, cols], keys_t, preferred_element_type=jnp.float32) * factor
            scores = jnp.where(key_open, scores, -1e30)
            row_max = jnp.max(scores, axis=-1, keepdims=True)
            weights = jnp.exp(scores - row_max) * live
            probs = (weights / jnp.sum(weights, axis=-1, keepdims=True)).astype(jnp.bfloat16)
            att = jnp.dot(probs, values, preferred_element_type=jnp.float32)
            o_ref[rows, cols] = att.astype(o_ref.dtype)


def attend(flat_idx, queries, slots, live, entry_len):
    tok_rows, head_cols = queries.shape
    segment_count = flat_idx.shape[0] // NBRS
    seg_rows = tok_rows // segment_count
    slot_rows, kv_cols = slots.shape[1], slots.shape[2]
    per_step = NBRS * SEGS_PER_STEP

    def kv_spec(j):
        return pl.BlockSpec((1, slot_rows, kv_cols), lambda s, f: (f[s * per_step + j], 0, 0))

    grid_spec = pltpu.PrefetchScalarGridSpec(
        num_scalar_prefetch=1,
        grid=(segment_count // SEGS_PER_STEP,),
        in_specs=[pl.BlockSpec((seg_rows * SEGS_PER_STEP, head_cols), lambda s, f: (s, 0))]
        + [kv_spec(j) for j in range(per_step)]
        + [pl.BlockSpec((SEGS_PER_STEP, 1, live.shape[2]), lambda s, f: (s, 0, 0))],
        out_specs=pl.BlockSpec((seg_rows * SEGS_PER_STEP, head_cols), lambda s, f: (s, 0)),
    )
    return pl.pallas_call(
        functools.partial(attend_kernel, entry_len=entry_len),
        out_shape=jax.ShapeDtypeStruct((tok_rows, head_cols), jnp.bfloat16),
        grid_spec=grid_spec,
    )(flat_idx, queries, *([slots] * per_step), live)


def local(dp_count, retr_count, tensor_count, hidden_in, norm_gain, nbr_table, encodings, enc_mask, w_query, w_key, w_value, w_out):
    segment_count = nbr_table.shape[0]
    nb_dev, entry_len, enc_width = encodings.shape
    mask_cols = enc_mask.shape[1]
    head_cols = w_key.shape[1]
    wanted = nbr_table.reshape(-1)
    need_count = wanted.shape[0]

    feat = hidden_in.shape[1]
    t = lax.axis_index("tensor")
    fwd = [(i, (i + 1) % tensor_count) for i in range(tensor_count)]
    bwd = [(i, (i - 1) % tensor_count) for i in range(tensor_count)]
    pieces = [(0, hidden_in)]
    up = down = hidden_in
    half_ring = tensor_count // 2
    for k in range(1, half_ring):
        up = lax.ppermute(up, "tensor", fwd)
        down = lax.ppermute(down, "tensor", bwd)
        pieces.append((k, up))
        pieces.append((tensor_count - k, down))
    half_rows = hidden_in.shape[0] // 2
    top = lax.ppermute(up[:half_rows], "tensor", fwd)
    bottom = lax.ppermute(down[half_rows:], "tensor", bwd)
    pieces.append((half_ring, jnp.concatenate([top, bottom], axis=0)))

    per_dev = nb_dev
    enc_half = encodings
    mask_half = enc_mask
    w_both = jnp.concatenate([w_key, w_value], axis=1)
    own_kv = jnp.dot(
        enc_half.reshape(per_dev * entry_len, enc_width), w_both, preferred_element_type=jnp.float32
    ).astype(jnp.bfloat16).reshape(per_dev, entry_len, 2 * head_cols)
    head_count = head_cols // HD
    keys_t = own_kv[:, :, :head_cols].reshape(per_dev, entry_len, head_count, HD)
    keys_t = keys_t.transpose(0, 3, 2, 1).reshape(per_dev, HD, head_count * entry_len)
    own_kv = jnp.concatenate([keys_t, own_kv[:, :, head_cols:]], axis=2)
    slots = lax.all_gather(own_kv, "retr", axis=0, tiled=True)
    slot_of = wanted
    mask_copies = jnp.broadcast_to(mask_half[None], (retr_count,) + mask_half.shape)
    all_marks = lax.all_to_all(mask_copies, "retr", 0, 0, tiled=True)
    all_marks = all_marks.reshape(retr_count * nb_dev, mask_cols)
    key_live = jnp.repeat(jnp.take(all_marks, wanted, axis=0), BLOCK, axis=1)
    key_live = key_live.astype(jnp.float32).reshape(segment_count, 1, NBRS * entry_len)

    widened = [p.astype(jnp.float32) for _, p in pieces]
    sum_sq = sum(jnp.sum(w * w, axis=-1, keepdims=True) for w in widened)
    inv = lax.rsqrt(sum_sq / (feat * tensor_count) + 1e-05)
    acc = None
    for (k, _), w in zip(pieces, widened):
        src_block = (t - k) % tensor_count
        gain = lax.dynamic_slice_in_dim(norm_gain, src_block * feat, feat)
        normed = (w * inv * gain).astype(jnp.bfloat16)
        w_rows = lax.dynamic_slice_in_dim(w_query, src_block * feat, feat, axis=0)
        part = jnp.dot(normed, w_rows, preferred_element_type=jnp.float32)
        acc = part if acc is None else acc + part
    queries = acc.astype(jnp.bfloat16)

    attended = attend(slot_of, queries, slots, key_live, entry_len)
    partial_value = jnp.dot(attended, w_out, preferred_element_type=jnp.float32)
    summed = lax.psum_scatter(
        partial_value.astype(jnp.bfloat16), "tensor", scatter_dimension=1, tiled=True
    )
    return (hidden_in.astype(jnp.float32) + summed.astype(jnp.float32)).astype(jnp.bfloat16)


def solution(mesh):
    in_specs = (
        P(("dp", "retr"), "tensor"),
        P(),
        P(("dp", "retr"), None),
        P("retr", None, None),
        P("retr", None),
        P(None, "tensor"),
        P(None, "tensor"),
        P(None, "tensor"),
        P("tensor", None),
    )
    out_specs = P(("dp", "retr"), "tensor")
    body = functools.partial(local, mesh.shape["dp"], mesh.shape["retr"], mesh.shape["tensor"])
    return jax.shard_map(body, mesh=mesh, in_specs=in_specs, out_specs=out_specs, check_vma=False)
```

```python
import functools
import math

import jax
import jax.numpy as jnp
from jax import lax
from jax.experimental import pallas as pl
from jax.experimental.pallas import tpu as pltpu
from jax.sharding import PartitionSpec as P

HD = 128
NBRS = 2
BLOCK = 32
CAP = 2
SEGS_PER_STEP = 4


def attend_kernel(flat_ref, q_ref, *refs, entry_len):
    kv_refs, live_ref, o_ref = refs[:-2], refs[-2], refs[-1]
    head_cols = q_ref.shape[1]
    seg_rows = q_ref.shape[0] // SEGS_PER_STEP
    factor = 1.0 / math.sqrt(HD)
    for g in range(SEGS_PER_STEP):
        kv0_ref, kv1_ref = kv_refs[g * NBRS], kv_refs[g * NBRS + 1]
        rows = slice(g * seg_rows, (g + 1) * seg_rows)
        live = live_ref[g]
        key_open = live > 0
        for h in range(head_cols // HD):
            cols = slice(h * HD, (h + 1) * HD)
            vcols = slice(head_cols + h * HD, head_cols + (h + 1) * HD)
            kcols = slice(h * entry_len, (h + 1) * entry_len)
            keys_t = jnp.concatenate([kv0_ref[0, :HD, kcols], kv1_ref[0, :HD, kcols]], axis=1)
            values = jnp.concatenate(
                [kv0_ref[0, :entry_len, vcols], kv1_ref[0, :entry_len, vcols]], axis=0
            )
            scores = jnp.dot(q_ref[rows, cols], keys_t, preferred_element_type=jnp.float32) * factor
            scores = jnp.where(key_open, scores, -1e30)
            row_max = jnp.max(scores, axis=-1, keepdims=True)
            weights = jnp.exp(scores - row_max) * live
            probs = (weights / jnp.sum(weights, axis=-1, keepdims=True)).astype(jnp.bfloat16)
            att = jnp.dot(probs, values, preferred_element_type=jnp.float32)
            o_ref[rows, cols] = att.astype(o_ref.dtype)


def attend(flat_idx, queries, slots, live, entry_len):
    tok_rows, head_cols = queries.shape
    segment_count = flat_idx.shape[0] // NBRS
    seg_rows = tok_rows // segment_count
    slot_rows, kv_cols = slots.shape[1], slots.shape[2]
    per_step = NBRS * SEGS_PER_STEP

    def kv_spec(j):
        return pl.BlockSpec((1, slot_rows, kv_cols), lambda s, f: (f[s * per_step + j], 0, 0))

    grid_spec = pltpu.PrefetchScalarGridSpec(
        num_scalar_prefetch=1,
        grid=(segment_count // SEGS_PER_STEP,),
        in_specs=[pl.BlockSpec((seg_rows * SEGS_PER_STEP, head_cols), lambda s, f: (s, 0))]
        + [kv_spec(j) for j in range(per_step)]
        + [pl.BlockSpec((SEGS_PER_STEP, 1, live.shape[2]), lambda s, f: (s, 0, 0))],
        out_specs=pl.BlockSpec((seg_rows * SEGS_PER_STEP, head_cols), lambda s, f: (s, 0)),
    )
    return pl.pallas_call(
        functools.partial(attend_kernel, entry_len=entry_len),
        out_shape=jax.ShapeDtypeStruct((tok_rows, head_cols), jnp.bfloat16),
        grid_spec=grid_spec,
    )(flat_idx, queries, *([slots] * per_step), live)


def local(dp_count, retr_count, tensor_count, hidden_in, norm_gain, nbr_table, encodings, enc_mask, w_query, w_key, w_value, w_out):
    segment_count = nbr_table.shape[0]
    nb_dev, entry_len, enc_width = encodings.shape
    mask_cols = enc_mask.shape[1]
    head_cols = w_key.shape[1]
    wanted = nbr_table.reshape(-1)
    need_count = wanted.shape[0]

    feat = hidden_in.shape[1]
    t = lax.axis_index("tensor")
    fwd = [(i, (i + 1) % tensor_count) for i in range(tensor_count)]
    bwd = [(i, (i - 1) % tensor_count) for i in range(tensor_count)]
    pieces = [(0, hidden_in)]
    up = down = hidden_in
    half_ring = tensor_count // 2
    for k in range(1, half_ring):
        up = lax.ppermute(up, "tensor", fwd)
        down = lax.ppermute(down, "tensor", bwd)
        pieces.append((k, up))
        pieces.append((tensor_count - k, down))
    half_rows = hidden_in.shape[0] // 2
    top = lax.ppermute(up[:half_rows], "tensor", fwd)
    bottom = lax.ppermute(down[half_rows:], "tensor", bwd)
    pieces.append((half_ring, jnp.concatenate([top, bottom], axis=0)))

    per_dev = nb_dev
    enc_half = encodings
    mask_half = enc_mask
    w_both = jnp.concatenate([w_key, w_value], axis=1)
    own_kv = jnp.dot(
        enc_half.reshape(per_dev * entry_len, enc_width), w_both, preferred_element_type=jnp.float32
    ).astype(jnp.bfloat16).reshape(per_dev, entry_len, 2 * head_cols)
    head_count = head_cols // HD
    keys_t = own_kv[:, :, :head_cols].reshape(per_dev, entry_len, head_count, HD)
    keys_t = keys_t.transpose(0, 3, 2, 1).reshape(per_dev, HD, head_count * entry_len)
    own_kv = jnp.concatenate([keys_t, own_kv[:, :, head_cols:]], axis=2)
    slots = lax.all_gather(own_kv, "retr", axis=0, tiled=True)
    slot_of = wanted
    mask_copies = jnp.broadcast_to(mask_half[None], (retr_count,) + mask_half.shape)
    all_marks = lax.all_to_all(mask_copies, "retr", 0, 0, tiled=True)
    all_marks = all_marks.reshape(retr_count * nb_dev, mask_cols)
    key_live = jnp.repeat(jnp.take(all_marks, wanted, axis=0), BLOCK, axis=1)
    key_live = key_live.astype(jnp.float32).reshape(segment_count, 1, NBRS * entry_len)

    widened = [p.astype(jnp.float32) for _, p in pieces]
    sum_sq = sum(jnp.sum(w * w, axis=-1, keepdims=True) for w in widened)
    inv = lax.rsqrt(sum_sq / (feat * tensor_count) + 1e-05)
    acc = None
    for (k, _), w in zip(pieces, widened):
        src_block = (t - k) % tensor_count
        gain = lax.dynamic_slice_in_dim(norm_gain, src_block * feat, feat)
        normed = (w * inv * gain).astype(jnp.bfloat16)
        w_rows = lax.dynamic_slice_in_dim(w_query, src_block * feat, feat, axis=0)
        part = jnp.dot(normed, w_rows, preferred_element_type=jnp.float32)
        acc = part if acc is None else acc + part
    queries = acc.astype(jnp.bfloat16)

    attended = attend(slot_of, queries, slots, key_live, entry_len)
    partial_value = jnp.dot(attended, w_out, preferred_element_type=jnp.float32)
    summed = lax.psum_scatter(
        partial_value.astype(jnp.bfloat16), "tensor", scatter_dimension=1, tiled=True
    )
    return (hidden_in.astype(jnp.float32) + summed.astype(jnp.float32)).astype(jnp.bfloat16)


def solution(mesh):
    in_specs = (
        P(("dp", "retr"), "tensor"),
        P(),
        P(("dp", "retr"), None),
        P("retr", None, None),
        P("retr", None),
        P(None, "tensor"),
        P(None, "tensor"),
        P(None, "tensor"),
        P("tensor", None),
    )
    out_specs = P(("dp", "retr"), "tensor")
    body = functools.partial(local, mesh.shape["dp"], mesh.shape["retr"], mesh.shape["tensor"])
    return jax.shard_map(body, mesh=mesh, in_specs=in_specs, out_specs=out_specs, check_vma=False)
```

```python
import functools
import math

import jax
import jax.numpy as jnp
from jax import lax
from jax.experimental import pallas as pl
from jax.experimental.pallas import tpu as pltpu
from jax.sharding import PartitionSpec as P

HD = 128
NBRS = 2
BLOCK = 32
CAP = 2
SEGS_PER_STEP = 4


def attend_kernel(flat_ref, q_ref, *refs, entry_len):
    kv_refs, live_ref, o_ref = refs[:-2], refs[-2], refs[-1]
    head_cols = q_ref.shape[1]
    seg_rows = q_ref.shape[0] // SEGS_PER_STEP
    factor = 1.0 / math.sqrt(HD)
    for g in range(SEGS_PER_STEP):
        kv0_ref, kv1_ref = kv_refs[g * NBRS], kv_refs[g * NBRS + 1]
        rows = slice(g * seg_rows, (g + 1) * seg_rows)
        live = live_ref[g]
        key_open = live > 0
        for h in range(head_cols // HD):
            cols = slice(h * HD, (h + 1) * HD)
            vcols = slice(head_cols + h * HD, head_cols + (h + 1) * HD)
            kcols = slice(h * entry_len, (h + 1) * entry_len)
            keys_t = jnp.concatenate([kv0_ref[0, :HD, kcols], kv1_ref[0, :HD, kcols]], axis=1)
            values = jnp.concatenate(
                [kv0_ref[0, :entry_len, vcols], kv1_ref[0, :entry_len, vcols]], axis=0
            )
            scores = jnp.dot(q_ref[rows, cols], keys_t, preferred_element_type=jnp.float32) * factor
            scores = jnp.where(key_open, scores, -1e30)
            row_max = jnp.max(scores, axis=-1, keepdims=True)
            weights = jnp.exp(scores - row_max) * live
            probs = (weights / jnp.sum(weights, axis=-1, keepdims=True)).astype(jnp.bfloat16)
            att = jnp.dot(probs, values, preferred_element_type=jnp.float32)
            o_ref[rows, cols] = att.astype(o_ref.dtype)


def attend(flat_idx, queries, slots, live, entry_len):
    tok_rows, head_cols = queries.shape
    segment_count = flat_idx.shape[0] // NBRS
    seg_rows = tok_rows // segment_count
    slot_rows, kv_cols = slots.shape[1], slots.shape[2]
    per_step = NBRS * SEGS_PER_STEP

    def kv_spec(j):
        return pl.BlockSpec((1, slot_rows, kv_cols), lambda s, f: (f[s * per_step + j], 0, 0))

    grid_spec = pltpu.PrefetchScalarGridSpec(
        num_scalar_prefetch=1,
        grid=(segment_count // SEGS_PER_STEP,),
        in_specs=[pl.BlockSpec((seg_rows * SEGS_PER_STEP, head_cols), lambda s, f: (s, 0))]
        + [kv_spec(j) for j in range(per_step)]
        + [pl.BlockSpec((SEGS_PER_STEP, 1, live.shape[2]), lambda s, f: (s, 0, 0))],
        out_specs=pl.BlockSpec((seg_rows * SEGS_PER_STEP, head_cols), lambda s, f: (s, 0)),
    )
    return pl.pallas_call(
        functools.partial(attend_kernel, entry_len=entry_len),
        out_shape=jax.ShapeDtypeStruct((tok_rows, head_cols), jnp.bfloat16),
        grid_spec=grid_spec,
    )(flat_idx, queries, *([slots] * per_step), live)


def local(dp_count, retr_count, tensor_count, hidden_in, norm_gain, nbr_table, encodings, enc_mask, w_query, w_key, w_value, w_out):
    segment_count = nbr_table.shape[0]
    nb_dev, entry_len, enc_width = encodings.shape
    mask_cols = enc_mask.shape[1]
    head_cols = w_key.shape[1]
    wanted = nbr_table.reshape(-1)
    need_count = wanted.shape[0]

    feat = hidden_in.shape[1]
    t = lax.axis_index("tensor")
    fwd = [(i, (i + 1) % tensor_count) for i in range(tensor_count)]
    bwd = [(i, (i - 1) % tensor_count) for i in range(tensor_count)]
    pieces = [(0, hidden_in)]
    up = down = hidden_in
    half_ring = tensor_count // 2
    for k in range(1, half_ring):
        up = lax.ppermute(up, "tensor", fwd)
        down = lax.ppermute(down, "tensor", bwd)
        pieces.append((k, up))
        pieces.append((tensor_count - k, down))
    half_rows = hidden_in.shape[0] // 2
    top = lax.ppermute(up[:half_rows], "tensor", fwd)
    bottom = lax.ppermute(down[half_rows:], "tensor", bwd)
    pieces.append((half_ring, jnp.concatenate([top, bottom], axis=0)))

    per_dev = nb_dev
    enc_half = encodings
    mask_half = enc_mask
    w_both = jnp.concatenate([w_key, w_value], axis=1)
    own_kv = jnp.dot(
        enc_half.reshape(per_dev * entry_len, enc_width), w_both, preferred_element_type=jnp.float32
    ).astype(jnp.bfloat16).reshape(per_dev, entry_len, 2 * head_cols)
    head_count = head_cols // HD
    keys_t = own_kv[:, :, :head_cols].reshape(per_dev, entry_len, head_count, HD)
    keys_t = keys_t.transpose(0, 3, 2, 1).reshape(per_dev, HD, head_count * entry_len)
    own_kv = jnp.concatenate([keys_t, own_kv[:, :, head_cols:]], axis=2)
    slots = lax.all_gather(own_kv, "retr", axis=0, tiled=True)
    slot_of = wanted
    mask_copies = jnp.broadcast_to(mask_half[None], (retr_count,) + mask_half.shape)
    all_marks = lax.all_to_all(mask_copies, "retr", 0, 0, tiled=True)
    all_marks = all_marks.reshape(retr_count * nb_dev, mask_cols)
    key_live = jnp.repeat(jnp.take(all_marks, wanted, axis=0), BLOCK, axis=1)
    key_live = key_live.astype(jnp.float32).reshape(segment_count, 1, NBRS * entry_len)

    widened = [p.astype(jnp.float32) for _, p in pieces]
    sum_sq = sum(jnp.sum(w * w, axis=-1, keepdims=True) for w in widened)
    inv = lax.rsqrt(sum_sq / (feat * tensor_count) + 1e-05)
    acc = None
    for (k, _), w in zip(pieces, widened):
        src_block = (t - k) % tensor_count
        gain = lax.dynamic_slice_in_dim(norm_gain, src_block * feat, feat)
        normed = (w * inv * gain).astype(jnp.bfloat16)
        w_rows = lax.dynamic_slice_in_dim(w_query, src_block * feat, feat, axis=0)
        part = jnp.dot(normed, w_rows, preferred_element_type=jnp.float32)
        acc = part if acc is None else acc + part
    queries = acc.astype(jnp.bfloat16)

    attended = attend(slot_of, queries, slots, key_live, entry_len)
    partial_value = jnp.dot(attended, w_out, preferred_element_type=jnp.float32)
    own_block = lax.dynamic_slice_in_dim(partial_value, t * feat, feat, axis=1)
    partial_value = lax.dynamic_update_slice_in_dim(
        partial_value, own_block + hidden_in.astype(jnp.float32), t * feat, axis=1
    )
    return lax.psum_scatter(
        partial_value.astype(jnp.bfloat16), "tensor", scatter_dimension=1, tiled=True
    )


def solution(mesh):
    in_specs = (
        P(("dp", "retr"), "tensor"),
        P(),
        P(("dp", "retr"), None),
        P("retr", None, None),
        P("retr", None),
        P(None, "tensor"),
        P(None, "tensor"),
        P(None, "tensor"),
        P("tensor", None),
    )
    out_specs = P(("dp", "retr"), "tensor")
    body = functools.partial(local, mesh.shape["dp"], mesh.shape["retr"], mesh.shape["tensor"])
    return jax.shard_map(body, mesh=mesh, in_specs=in_specs, out_specs=out_specs, check_vma=False)
```

```python
import functools
import math

import jax
import jax.numpy as jnp
from jax import lax
from jax.experimental import pallas as pl
from jax.experimental.pallas import tpu as pltpu
from jax.sharding import PartitionSpec as P

HD = 128
NBRS = 2
BLOCK = 32
CAP = 2
SEGS_PER_STEP = 4


def attend_kernel(flat_ref, q_ref, *refs, entry_len):
    kv_refs, live_ref, o_ref = refs[:-2], refs[-2], refs[-1]
    head_cols = q_ref.shape[1]
    seg_rows = q_ref.shape[0] // SEGS_PER_STEP
    factor = 1.0 / math.sqrt(HD)
    for g in range(SEGS_PER_STEP):
        kv0_ref, kv1_ref = kv_refs[g * NBRS], kv_refs[g * NBRS + 1]
        rows = slice(g * seg_rows, (g + 1) * seg_rows)
        live = live_ref[g]
        key_open = live > 0
        for h in range(head_cols // HD):
            cols = slice(h * HD, (h + 1) * HD)
            vcols = slice(head_cols + h * HD, head_cols + (h + 1) * HD)
            kcols = slice(h * entry_len, (h + 1) * entry_len)
            keys_t = jnp.concatenate([kv0_ref[0, :HD, kcols], kv1_ref[0, :HD, kcols]], axis=1)
            values = jnp.concatenate(
                [kv0_ref[0, :entry_len, vcols], kv1_ref[0, :entry_len, vcols]], axis=0
            )
            scores = jnp.dot(q_ref[rows, cols], keys_t, preferred_element_type=jnp.float32) * factor
            scores = jnp.where(key_open, scores, -1e30)
            row_max = jnp.max(scores, axis=-1, keepdims=True)
            weights = jnp.exp(scores - row_max) * live
            probs = (weights / jnp.sum(weights, axis=-1, keepdims=True)).astype(jnp.bfloat16)
            att = jnp.dot(probs, values, preferred_element_type=jnp.float32)
            o_ref[rows, cols] = att.astype(o_ref.dtype)


def attend(flat_idx, queries, slots, live, entry_len):
    tok_rows, head_cols = queries.shape
    segment_count = flat_idx.shape[0] // NBRS
    seg_rows = tok_rows // segment_count
    slot_rows, kv_cols = slots.shape[1], slots.shape[2]
    per_step = NBRS * SEGS_PER_STEP

    def kv_spec(j):
        return pl.BlockSpec((1, slot_rows, kv_cols), lambda s, f: (f[s * per_step + j], 0, 0))

    grid_spec = pltpu.PrefetchScalarGridSpec(
        num_scalar_prefetch=1,
        grid=(segment_count // SEGS_PER_STEP,),
        in_specs=[pl.BlockSpec((seg_rows * SEGS_PER_STEP, head_cols), lambda s, f: (s, 0))]
        + [kv_spec(j) for j in range(per_step)]
        + [pl.BlockSpec((SEGS_PER_STEP, 1, live.shape[2]), lambda s, f: (s, 0, 0))],
        out_specs=pl.BlockSpec((seg_rows * SEGS_PER_STEP, head_cols), lambda s, f: (s, 0)),
    )
    return pl.pallas_call(
        functools.partial(attend_kernel, entry_len=entry_len),
        out_shape=jax.ShapeDtypeStruct((tok_rows, head_cols), jnp.bfloat16),
        grid_spec=grid_spec,
    )(flat_idx, queries, *([slots] * per_step), live)


def local(dp_count, retr_count, tensor_count, hidden_in, norm_gain, nbr_table, encodings, enc_mask, w_query, w_key, w_value, w_out):
    segment_count = nbr_table.shape[0]
    nb_dev, entry_len, enc_width = encodings.shape
    mask_cols = enc_mask.shape[1]
    head_cols = w_key.shape[1]
    wanted = nbr_table.reshape(-1)
    need_count = wanted.shape[0]

    feat = hidden_in.shape[1]
    t = lax.axis_index("tensor")
    fwd = [(i, (i + 1) % tensor_count) for i in range(tensor_count)]
    bwd = [(i, (i - 1) % tensor_count) for i in range(tensor_count)]
    pieces = [(0, hidden_in)]
    up = down = hidden_in
    half_ring = tensor_count // 2
    for k in range(1, half_ring):
        up = lax.ppermute(up, "tensor", fwd)
        down = lax.ppermute(down, "tensor", bwd)
        pieces.append((k, up))
        pieces.append((tensor_count - k, down))
    half_rows = hidden_in.shape[0] // 2
    top = lax.ppermute(up[:half_rows], "tensor", fwd)
    bottom = lax.ppermute(down[half_rows:], "tensor", bwd)
    pieces.append((half_ring, jnp.concatenate([top, bottom], axis=0)))

    per_dev = nb_dev
    enc_half = encodings
    mask_half = enc_mask
    enc_flat = enc_half.reshape(per_dev * entry_len, enc_width)
    own_k = jnp.dot(enc_flat, w_key, preferred_element_type=jnp.float32).astype(jnp.bfloat16)
    own_v = jnp.dot(enc_flat, w_value, preferred_element_type=jnp.float32).astype(jnp.bfloat16)
    head_count = head_cols // HD
    keys_t = own_k.reshape(per_dev, entry_len, head_count, HD)
    keys_t = keys_t.transpose(0, 3, 2, 1).reshape(per_dev, HD, head_count * entry_len)
    own_kv = jnp.concatenate([keys_t, own_v.reshape(per_dev, entry_len, head_cols)], axis=2)
    slots = lax.all_gather(own_kv, "retr", axis=0, tiled=True)
    slot_of = wanted
    mask_copies = jnp.broadcast_to(mask_half[None], (retr_count,) + mask_half.shape)
    all_marks = lax.all_to_all(mask_copies, "retr", 0, 0, tiled=True)
    all_marks = all_marks.reshape(retr_count * nb_dev, mask_cols)
    key_live = jnp.repeat(jnp.take(all_marks, wanted, axis=0), BLOCK, axis=1)
    key_live = key_live.astype(jnp.float32).reshape(segment_count, 1, NBRS * entry_len)

    widened = [p.astype(jnp.float32) for _, p in pieces]
    sum_sq = sum(jnp.sum(w * w, axis=-1, keepdims=True) for w in widened)
    inv = lax.rsqrt(sum_sq / (feat * tensor_count) + 1e-05)
    acc = None
    for (k, _), w in zip(pieces, widened):
        src_block = (t - k) % tensor_count
        gain = lax.dynamic_slice_in_dim(norm_gain, src_block * feat, feat)
        normed = (w * inv * gain).astype(jnp.bfloat16)
        w_rows = lax.dynamic_slice_in_dim(w_query, src_block * feat, feat, axis=0)
        part = jnp.dot(normed, w_rows, preferred_element_type=jnp.float32)
        acc = part if acc is None else acc + part
    queries = acc.astype(jnp.bfloat16)

    attended = attend(slot_of, queries, slots, key_live, entry_len)
    partial_value = jnp.dot(attended, w_out, preferred_element_type=jnp.float32)
    summed = lax.psum_scatter(
        partial_value.astype(jnp.bfloat16), "tensor", scatter_dimension=1, tiled=True
    )
    return (hidden_in.astype(jnp.float32) + summed.astype(jnp.float32)).astype(jnp.bfloat16)


def solution(mesh):
    in_specs = (
        P(("dp", "retr"), "tensor"),
        P(),
        P(("dp", "retr"), None),
        P("retr", None, None),
        P("retr", None),
        P(None, "tensor"),
        P(None, "tensor"),
        P(None, "tensor"),
        P("tensor", None),
    )
    out_specs = P(("dp", "retr"), "tensor")
    body = functools.partial(local, mesh.shape["dp"], mesh.shape["retr"], mesh.shape["tensor"])
    return jax.shard_map(body, mesh=mesh, in_specs=in_specs, out_specs=out_specs, check_vma=False)
```
